512 devices in a mesh: req: 64 (over y_hi, z, core), tp: 8 (over y_lo, x).
Axes of the slice: x: 4, y: 4 (y_hi: 2, y_lo: 2; y = y_hi * 2 + y_lo), z: 16, core: 2. Of those that a mesh axis runs over, the one named last changes fastest.
Arguments:
- tokens: bfloat16 [64, 512, 2048], P('req', 'tp'), may hold values from -6 to 6
- w_q: bfloat16 [2048, 1024], P(None, 'tp')
- w_k: bfloat16 [2048, 1024], P(None, 'tp')
- w_v: bfloat16 [2048, 1024], P(None, 'tp'), may hold values from -0.125 to 0.125
- w_o: bfloat16 [1024, 2048], P('tp'), may hold values from -0.1875 to 0.1875
- q_gain: float32 [1024], P('tp'), may hold values from 0.1 to 1.9
- k_gain: float32 [1024], P('tp'), may hold values from 0.1 to 1.9
- out_gain: float32 [2048], replicated, may hold values from 0.1 to 1.9
- cache_lens: int32 [64], P('req'), may hold values from 512 to 4096, as said below
- group_ids: int32 [64], replicated, may hold values from 0 to 7
- prefix_cache: bfloat16 [8, 1024, 2048], P(None, 'req', 'tp'), may hold values from -6 to 6
- cache_rows: bfloat16 [64, 4096, 2048], P('req', None, 'tp'), may hold values from -105 to 105
Outputs:
- hidden: bfloat16 [64, 512, 2048], P('req', 'tp')
- appended: bfloat16 [64, 512, 2048], P('req', None, 'tp')
The draws below stay inside these ranges and needn't reach their ends.
Inputs may be any that keep to these rules, and one draw needn't show every extreme that they name: `cache_lens`: every draw holds a request with exactly 4096 cached positions.
All inputs are finite; a program needn't handle non-finite values.
Results may differ from the reference program's by a relative error of at most 0.013.
Values may be sent and summed in bfloat16 or wider, within the bound.
No kernel may reach another device: no remote copies, remote signals or barrier semaphores. Data moves between devices by JAX's collectives and lax.ppermute only.
A program may use at most 64 MiB of HBM per device.

```python
import jax
import jax.numpy as jnp
from jax import lax

D = 2048
HEADS = 8
HD = 128
GROUPS = 8
NEW = 512
CMAX = 4096
PREFIX = 1024
REQS = 64
N_TP = 8


def head_ramp():
    return jnp.repeat(0.6 * jnp.power(3.0, jnp.arange(HEADS, dtype=jnp.float32) / (HEADS - 1)), HD)


def ramped_weight(key):
    base = jax.random.normal(key, (D, HEADS * HD), jnp.float32)
    return (base * D ** (-0.5) * head_ramp()[None, :]).astype(jnp.bfloat16)


def draw_w_q(key, part):
    return ramped_weight(jax.random.fold_in(key, 11))


def draw_w_k(key, part):
    return ramped_weight(jax.random.fold_in(key, 12))


def draw_cache_lens(key, part):
    lens = jax.random.randint(jax.random.fold_in(key, 21), (REQS,), CMAX // 8, CMAX + 1)
    spot = jax.random.randint(jax.random.fold_in(key, 22), (), 0, REQS)
    return lens.at[spot].set(CMAX).astype(jnp.int32)


def draw_cache_rows(key, part):
    full_shape = (REQS, CMAX, HEADS, 2, HD)
    subkey = jax.random.fold_in(key, 31)
    base = jnp.clip(jax.random.normal(subkey, full_shape, jnp.float32), -6.0, 6.0)
    return base.reshape(REQS, CMAX, HEADS * 2 * HD).astype(jnp.bfloat16)


def touch_ends(array, own_key, least, top_value):
    place = [jax.random.randint(jax.random.fold_in(own_key, axis), (), 0, length) for axis, length in enumerate(array.shape)]
    main_axis = array.shape.index(max(array.shape))
    beside = place[:main_axis] + [(place[main_axis] + 1) % array.shape[main_axis]] + place[main_axis + 1:]
    return array.at[tuple(place)].set(least).at[tuple(beside)].set(top_value)


def level_of(key, extent, pieces, low, top_value):
    def one(position, shards_of):
        steps = jax.random.uniform(jax.random.fold_in(jax.random.fold_in(key, 6), position), (shards_of,), jnp.float32, low / len(pieces), top_value / len(pieces))
        return jnp.repeat(jnp.exp(steps), extent[position] // shards_of).reshape((-1,) + (1,) * (len(extent) - position - 1))

    factor_of = one(*pieces[0])
    for cut in pieces[1:]:
        factor_of = factor_of * one(*cut)
    return factor_of


def gaussian(stream_key, extent, width, most, cuts=(), kind=jnp.bfloat16):
    array = width * jax.random.normal(stream_key, extent, jnp.float32)
    if cuts:
        array = array * level_of(stream_key, extent, cuts, -0.22, 0.18)
    return jnp.clip(array, -most, most).astype(kind)


def setup_inputs(seed: int = 0) -> dict:
    keys = jax.random.split(jax.random.key(seed), 13)
    tokens = gaussian(keys[0], (REQS, NEW, D), 1.0, 6.0, ((0, 64), (1, 8)))
    w_q = draw_w_q(jax.random.fold_in(keys[12], 71), 0)
    w_k = draw_w_k(jax.random.fold_in(keys[12], 71), 0)
    w_v = gaussian(keys[3], (D, HEADS * HD), D ** -0.5, 0.125, ((1, 8),))
    w_o = gaussian(keys[4], (HEADS * HD, D), (HEADS * HD) ** -0.5, 0.1875, ((0, 8),))
    q_gain = jnp.clip(1.0 + 0.18 * jax.random.normal(keys[5], (HEADS * HD,), jnp.float32), 0.1, 1.9)
    k_gain = jnp.clip(1.0 + 0.18 * jax.random.normal(keys[6], (HEADS * HD,), jnp.float32), 0.1, 1.9)
    out_gain = jnp.clip(1.0 + 0.18 * jax.random.normal(keys[7], (D,), jnp.float32), 0.1, 1.9)
    cache_lens = draw_cache_lens(jax.random.fold_in(keys[12], 71), 0)
    group_ids = touch_ends(jax.random.randint(keys[9], (REQS,), 0, GROUPS), jax.random.fold_in(keys[9], 1), 0, GROUPS - 1).astype(jnp.int32)
    prefix_cache = gaussian(keys[10], (GROUPS, PREFIX, HEADS * 2 * HD), 1.0, 6.0, ((1, 64), (2, 8)))
    cache_rows = draw_cache_rows(jax.random.fold_in(keys[12], 71), 0)
    return dict(tokens=tokens, w_q=w_q, w_k=w_k, w_v=w_v, w_o=w_o, q_gain=q_gain, k_gain=k_gain, out_gain=out_gain, cache_lens=cache_lens, group_ids=group_ids, prefix_cache=prefix_cache, cache_rows=cache_rows)


def rotate(values_in, positions):
    half_dim = values_in.shape[-1] // 2
    exponent = jnp.arange(half_dim, dtype=jnp.float32) * (-2.0 / values_in.shape[-1])
    inverse = jnp.power(jnp.float32(500000.0), exponent)
    angles = positions[:, None] * inverse[None, :]
    cosine = jnp.cos(angles)[:, None, :]
    sine_part = jnp.sin(angles)[:, None, :]
    first_half = values_in[..., :half_dim]
    second_half = values_in[..., half_dim:]
    return jnp.concatenate([first_half * cosine - second_half * sine_part, second_half * cosine + first_half * sine_part], -1)

def rms_scale(values_in, gain_vector):
    mean_sq = lax.optimization_barrier(jnp.mean(values_in * values_in, axis=-1, keepdims=True))
    return values_in * lax.rsqrt(mean_sq + 1e-06) * gain_vector

def reference(tokens, w_q, w_k, w_v, w_o, q_gain, k_gain, out_gain, cache_lens, group_ids, prefix_cache, cache_rows):
    score_scale = HD ** (-0.5)
    group_cols = HEADS // N_TP * HD

    def one_request(inputs):
        rows_in, length, group_id, cached = inputs
        queries = rms_scale(jnp.dot(rows_in, w_q, preferred_element_type=jnp.float32), q_gain)
        keys_new = rms_scale(jnp.dot(rows_in, w_k, preferred_element_type=jnp.float32), k_gain)
        values_new = jnp.dot(rows_in, w_v, preferred_element_type=jnp.float32)
        positions = (PREFIX + length + jnp.arange(NEW, dtype=jnp.int32)).astype(jnp.float32)
        q_rot = rotate(queries.reshape(NEW, HEADS, HD), positions).astype(jnp.bfloat16)
        k_rot = rotate(keys_new.reshape(NEW, HEADS, HD), positions).astype(jnp.bfloat16)
        v_new = values_new.reshape(NEW, HEADS, HD).astype(jnp.bfloat16)
        appended = jnp.stack([k_rot, v_new], axis=2).reshape(NEW, HEADS * 2 * HD)
        shared = lax.dynamic_index_in_dim(prefix_cache, group_id, 0, keepdims=False).reshape(PREFIX, HEADS, 2, HD)
        private = cached.reshape(CMAX, HEADS, 2, HD)
        keys_all = jnp.concatenate([shared[:, :, 0], private[:, :, 0], k_rot], 0)
        values_all = jnp.concatenate([shared[:, :, 1], private[:, :, 1], v_new], 0)
        query_pos = jnp.arange(NEW, dtype=jnp.int32)[:, None]
        cache_pos = jnp.arange(CMAX, dtype=jnp.int32)[None, :]
        visible = jnp.concatenate([jnp.ones((NEW, PREFIX), dtype=bool), jnp.broadcast_to(cache_pos < length, (NEW, CMAX)), jnp.arange(NEW, dtype=jnp.int32)[None, :] <= query_pos], 1)
        scores = jnp.einsum('qhd,khd->hqk', q_rot.astype(jnp.float32), keys_all.astype(jnp.float32)) * score_scale
        scores = jnp.where(visible[None], scores, -1e+30)
        row_peak = lax.optimization_barrier(jnp.max(scores, -1, keepdims=True))
        weights = jnp.where(visible[None], jnp.exp(scores - row_peak), 0.0)
        denominator = lax.optimization_barrier(jnp.sum(weights, -1))
        rounded = lax.optimization_barrier(weights.astype(jnp.bfloat16))
        mixed_heads = jnp.einsum('hqk,khd->hqd', rounded.astype(jnp.float32), values_all.astype(jnp.float32)) / denominator[..., None]
        attended = jnp.transpose(mixed_heads, (1, 0, 2)).reshape(NEW, HEADS * HD).astype(jnp.bfloat16)
        projected = jnp.zeros((NEW, D), jnp.float32)
        for group_index in range(N_TP):
            start = group_index * group_cols
            partial_value = jnp.dot(attended[:, start:start + group_cols], w_o[start:start + group_cols], preferred_element_type=jnp.float32)
            partial_value = lax.optimization_barrier(partial_value.astype(jnp.bfloat16))
            projected = projected + partial_value.astype(jnp.float32)
        hidden = (rows_in.astype(jnp.float32) + rms_scale(projected, out_gain)).astype(jnp.bfloat16)
        return (hidden, appended)
    hidden, appended = lax.map(one_request, (tokens, cache_lens, group_ids, cache_rows))
    return (hidden, appended)
```

```python
import jax
import jax.numpy as jnp
from jax import lax
from jax.sharding import PartitionSpec as P

HEADS = 8
HD = 128
NEW = 512


def rotate(values_in, positions):
    half_dim = values_in.shape[-1] // 2
    exponent = jnp.arange(half_dim, dtype=jnp.float32) * (-2.0 / values_in.shape[-1])
    inverse = jnp.power(jnp.float32(500000.0), exponent)
    angles = positions[:, None] * inverse[None, :]
    cosine = jnp.cos(angles)[:, None, :]
    sine_part = jnp.sin(angles)[:, None, :]
    first_half = values_in[..., :half_dim]
    second_half = values_in[..., half_dim:]
    return jnp.concatenate(
        [
            first_half * cosine - second_half * sine_part,
            second_half * cosine + first_half * sine_part,
        ],
        -1,
    )


def rms_scale(values_in, gain_vector):
    mean_sq = jnp.mean(values_in * values_in, axis=-1, keepdims=True)
    return values_in * lax.rsqrt(mean_sq + 1e-06) * gain_vector


def absorb(state_now, queries, keys_block, values_block, visible):
    running_max, denominator, weighted = state_now
    scores = jnp.einsum(
        "hqd,khd->hqk", queries, keys_block, preferred_element_type=jnp.float32
    ) * HD ** (-0.5)
    scores = jnp.where(visible[None], scores, -1e30)
    updated = jnp.maximum(running_max, jnp.max(scores, -1))
    factor = jnp.exp(running_max - updated)
    weights = jnp.where(visible[None], jnp.exp(scores - updated[..., None]), 0.0)
    denominator = denominator * factor + jnp.sum(weights, -1)
    weighted = weighted * factor[..., None] + jnp.einsum(
        "hqk,khd->hqd",
        weights.astype(jnp.bfloat16),
        values_block,
        preferred_element_type=jnp.float32,
    )
    return (updated, denominator, weighted)


def per_device(
    tokens,
    w_q,
    w_k,
    w_v,
    w_o,
    q_gain,
    k_gain,
    out_gain,
    cache_lens,
    group_ids,
    prefix_cache,
    cache_rows,
):
    heads_local = w_q.shape[1] // HD
    width_local = heads_local * HD
    flat_rows = lax.all_gather(tokens, "tp", axis=1, tiled=True)[0]
    projected = jnp.concatenate(
        [
            jnp.dot(flat_rows, w_q, preferred_element_type=jnp.float32)[None],
            jnp.dot(flat_rows, w_k, preferred_element_type=jnp.float32)[None],
            jnp.dot(flat_rows, w_v, preferred_element_type=jnp.float32)[None],
        ],
        axis=2,
    )[0]
    queries = projected[:, :width_local]
    keys_new = projected[:, width_local : 2 * width_local]
    values_new = projected[:, 2 * width_local :]
    square_sums = lax.psum((jnp.sum(queries * queries, -1), jnp.sum(keys_new * keys_new, -1)), "tp")
    full_width = HEADS * HD
    queries = queries * lax.rsqrt(square_sums[0] / full_width + 1e-06)[:, None] * q_gain
    keys_new = keys_new * lax.rsqrt(square_sums[1] / full_width + 1e-06)[:, None] * k_gain
    prefix_len = prefix_cache.shape[1] * lax.axis_size("req")
    length = cache_lens[0]
    positions = (prefix_len + length + jnp.arange(NEW, dtype=jnp.int32)).astype(jnp.float32)
    q_rot = rotate(queries.reshape(NEW, heads_local, HD), positions).astype(jnp.bfloat16)
    k_rot = rotate(keys_new.reshape(NEW, heads_local, HD), positions).astype(jnp.bfloat16)
    v_new = values_new.reshape(NEW, heads_local, HD).astype(jnp.bfloat16)
    appended = jnp.stack([k_rot, v_new], axis=2).reshape(1, NEW, heads_local * 2 * HD)
    q_heads = jnp.transpose(q_rot, (1, 0, 2))
    state_now = (
        jnp.full((heads_local, NEW), -1e30, jnp.float32),
        jnp.zeros((heads_local, NEW), jnp.float32),
        jnp.zeros((heads_local, NEW, HD), jnp.float32),
    )
    row_ids = jnp.arange(NEW, dtype=jnp.int32)
    state_now = absorb(state_now, q_heads, k_rot, v_new, row_ids[None, :] <= row_ids[:, None])
    cached = cache_rows[0]
    key_block = min(512, cached.shape[0])

    def cache_step(block_index, state_in):
        block = lax.dynamic_slice_in_dim(cached, block_index * key_block, key_block, 0).reshape(
            key_block, heads_local, 2, HD
        )
        columns = block_index * key_block + jnp.arange(key_block, dtype=jnp.int32)
        visible = jnp.broadcast_to(columns[None, :] < length, (NEW, key_block))
        return absorb(state_in, q_heads, block[:, :, 0], block[:, :, 1], visible)

    block_count = cached.shape[0] // key_block
    state_now = lax.fori_loop(0, block_count, cache_step, state_now)
    outgoing = jnp.take(prefix_cache, group_ids, axis=0)
    chosen = lax.all_to_all(outgoing, "req", 0, 0, tiled=True).reshape(-1, prefix_cache.shape[2])
    count = chosen.shape[0]
    chosen = chosen.reshape(count, heads_local, 2, HD)
    state_now = absorb(
        state_now, q_heads, chosen[:, :, 0], chosen[:, :, 1], jnp.ones((NEW, count), dtype=bool)
    )
    running_max, denominator, weighted = state_now
    attended = (
        jnp.transpose(weighted / denominator[..., None], (1, 0, 2))
        .reshape(NEW, width_local)
        .astype(jnp.bfloat16)
    )
    partial_out = jnp.dot(attended, w_o, preferred_element_type=jnp.float32)
    mine = lax.psum_scatter(
        partial_out.astype(jnp.bfloat16), "tp", scatter_dimension=0, tiled=True
    ).astype(jnp.float32)
    hidden = (tokens[0].astype(jnp.float32) + rms_scale(mine, out_gain)).astype(jnp.bfloat16)[None]
    return (hidden, appended)


def solution(mesh):
    return jax.shard_map(
        per_device,
        mesh=mesh,
        in_specs=(
            P("req", "tp", None),
            P(None, "tp"),
            P(None, "tp"),
            P(None, "tp"),
            P("tp", None),
            P("tp"),
            P("tp"),
            P(),
            P("req"),
            P(),
            P(None, "req", "tp"),
            P("req", None, "tp"),
        ),
        out_specs=(P("req", "tp", None), P("req", None, "tp")),
        check_vma=False,
    )
```

```python
import jax
import jax.numpy as jnp
from jax import lax
from jax.sharding import PartitionSpec as P

HEADS = 8
HD = 128
NEW = 512


def rotate(values_in, positions):
    half_dim = values_in.shape[-1] // 2
    exponent = jnp.arange(half_dim, dtype=jnp.float32) * (-2.0 / values_in.shape[-1])
    inverse = jnp.power(jnp.float32(500000.0), exponent)
    angles = positions[:, None] * inverse[None, :]
    cosine = jnp.cos(angles)[:, None, :]
    sine_part = jnp.sin(angles)[:, None, :]
    first_half = values_in[..., :half_dim]
    second_half = values_in[..., half_dim:]
    return jnp.concatenate(
        [
            first_half * cosine - second_half * sine_part,
            second_half * cosine + first_half * sine_part,
        ],
        -1,
    )


def rms_scale(values_in, gain_vector):
    mean_sq = jnp.mean(values_in * values_in, axis=-1, keepdims=True)
    return values_in * lax.rsqrt(mean_sq + 1e-06) * gain_vector


def absorb(state_now, queries, keys_block, values_block, visible):
    running_max, denominator, weighted = state_now
    scores = jnp.einsum(
        "hqd,khd->hqk", queries, keys_block, preferred_element_type=jnp.float32
    ) * HD ** (-0.5)
    scores = jnp.where(visible[None], scores, -1e30)
    updated = jnp.maximum(running_max, jnp.max(scores, -1))
    factor = jnp.exp(running_max - updated)
    weights = jnp.where(visible[None], jnp.exp(scores - updated[..., None]), 0.0)
    denominator = denominator * factor + jnp.sum(weights, -1)
    weighted = weighted * factor[..., None] + jnp.einsum(
        "hqk,khd->hqd",
        weights.astype(jnp.bfloat16),
        values_block,
        preferred_element_type=jnp.float32,
    )
    return (updated, denominator, weighted)


def per_device(
    tokens,
    w_q,
    w_k,
    w_v,
    w_o,
    q_gain,
    k_gain,
    out_gain,
    cache_lens,
    group_ids,
    prefix_cache,
    cache_rows,
):
    heads_local = w_q.shape[1] // HD
    width_local = heads_local * HD
    tp_size = lax.axis_size("tp")
    flat_rows = lax.all_to_all(
        jnp.broadcast_to(tokens, (tp_size,) + tokens.shape[1:]), "tp", 0, 0, tiled=True
    ).reshape(-1, tokens.shape[2])
    projected = jnp.concatenate(
        [
            jnp.dot(flat_rows, w_q, preferred_element_type=jnp.float32)[None],
            jnp.dot(flat_rows, w_k, preferred_element_type=jnp.float32)[None],
            jnp.dot(flat_rows, w_v, preferred_element_type=jnp.float32)[None],
        ],
        axis=2,
    )[0]
    queries = projected[:, :width_local]
    keys_new = projected[:, width_local : 2 * width_local]
    values_new = projected[:, 2 * width_local :]
    square_sums = lax.psum((jnp.sum(queries * queries, -1), jnp.sum(keys_new * keys_new, -1)), "tp")
    full_width = HEADS * HD
    queries = queries * lax.rsqrt(square_sums[0] / full_width + 1e-06)[:, None] * q_gain
    keys_new = keys_new * lax.rsqrt(square_sums[1] / full_width + 1e-06)[:, None] * k_gain
    prefix_len = prefix_cache.shape[1] * lax.axis_size("req")
    length = cache_lens[0]
    positions = (prefix_len + length + jnp.arange(NEW, dtype=jnp.int32)).astype(jnp.float32)
    q_rot = rotate(queries.reshape(NEW, heads_local, HD), positions).astype(jnp.bfloat16)
    k_rot = rotate(keys_new.reshape(NEW, heads_local, HD), positions).astype(jnp.bfloat16)
    v_new = values_new.reshape(NEW, heads_local, HD).astype(jnp.bfloat16)
    appended = jnp.stack([k_rot, v_new], axis=2).reshape(1, NEW, heads_local * 2 * HD)
    q_heads = jnp.transpose(q_rot, (1, 0, 2))
    state_now = (
        jnp.full((heads_local, NEW), -1e30, jnp.float32),
        jnp.zeros((heads_local, NEW), jnp.float32),
        jnp.zeros((heads_local, NEW, HD), jnp.float32),
    )
    row_ids = jnp.arange(NEW, dtype=jnp.int32)
    state_now = absorb(state_now, q_heads, k_rot, v_new, row_ids[None, :] <= row_ids[:, None])
    cached = cache_rows[0]
    key_block = min(512, cached.shape[0])

    def cache_step(block_index, state_in):
        block = lax.dynamic_slice_in_dim(cached, block_index * key_block, key_block, 0).reshape(
            key_block, heads_local, 2, HD
        )
        columns = block_index * key_block + jnp.arange(key_block, dtype=jnp.int32)
        visible = jnp.broadcast_to(columns[None, :] < length, (NEW, key_block))
        return absorb(state_in, q_heads, block[:, :, 0], block[:, :, 1], visible)

    block_count = cached.shape[0] // key_block
    state_now = lax.fori_loop(0, block_count, cache_step, state_now)
    outgoing = jnp.take(prefix_cache, group_ids, axis=0)
    chosen = lax.all_to_all(outgoing, "req", 0, 0, tiled=True).reshape(-1, prefix_cache.shape[2])
    count = chosen.shape[0]
    chosen = chosen.reshape(count, heads_local, 2, HD)
    state_now = absorb(
        state_now, q_heads, chosen[:, :, 0], chosen[:, :, 1], jnp.ones((NEW, count), dtype=bool)
    )
    running_max, denominator, weighted = state_now
    attended = (
        jnp.transpose(weighted / denominator[..., None], (1, 0, 2))
        .reshape(NEW, width_local)
        .astype(jnp.bfloat16)
    )
    partial_out = jnp.dot(attended, w_o, preferred_element_type=jnp.float32)
    blocks = partial_out.astype(jnp.bfloat16).reshape(tp_size, -1, partial_out.shape[1])
    mine = jnp.sum(lax.all_to_all(blocks, "tp", 0, 0, tiled=True).astype(jnp.float32), 0)
    hidden = (tokens[0].astype(jnp.float32) + rms_scale(mine, out_gain)).astype(jnp.bfloat16)[None]
    return (hidden, appended)


def solution(mesh):
    return jax.shard_map(
        per_device,
        mesh=mesh,
        in_specs=(
            P("req", "tp", None),
            P(None, "tp"),
            P(None, "tp"),
            P(None, "tp"),
            P("tp", None),
            P("tp"),
            P("tp"),
            P(),
            P("req"),
            P(),
            P(None, "req", "tp"),
            P("req", None, "tp"),
        ),
        out_specs=(P("req", "tp", None), P("req", None, "tp")),
        check_vma=False,
    )
```

```python
import functools

import jax
import jax.numpy as jnp
from jax import lax
from jax.sharding import PartitionSpec as P

HEADS = 8
HD = 128
NEW = 512


def rotate(values_in, positions):
    half_dim = values_in.shape[-1] // 2
    exponent = jnp.arange(half_dim, dtype=jnp.float32) * (-2.0 / values_in.shape[-1])
    inverse = jnp.power(jnp.float32(500000.0), exponent)
    angles = positions[:, None] * inverse[None, :]
    cosine = jnp.cos(angles)[:, None, :]
    sine_part = jnp.sin(angles)[:, None, :]
    first_half = values_in[..., :half_dim]
    second_half = values_in[..., half_dim:]
    return jnp.concatenate(
        [
            first_half * cosine - second_half * sine_part,
            second_half * cosine + first_half * sine_part,
        ],
        -1,
    )


def rms_scale(values_in, gain_vector):
    mean_sq = jnp.mean(values_in * values_in, axis=-1, keepdims=True)
    return values_in * lax.rsqrt(mean_sq + 1e-06) * gain_vector


def layer(
    tokens,
    w_q,
    w_k,
    w_v,
    w_o,
    q_gain,
    k_gain,
    out_gain,
    cache_lens,
    group_ids,
    prefix_cache,
    cache_rows,
):
    heads_local = w_q.shape[1] // HD
    width_local = heads_local * HD
    tp_size = lax.axis_size("tp")
    flat_rows = lax.all_to_all(
        jnp.broadcast_to(tokens, (tp_size,) + tokens.shape[1:]), "tp", 0, 0, tiled=True
    ).reshape(-1, tokens.shape[2])
    outgoing = jnp.take(prefix_cache, group_ids, axis=0)
    chosen = lax.all_to_all(outgoing, "req", 0, 0, tiled=True)
    queries = jnp.dot(flat_rows, w_q, preferred_element_type=jnp.float32)
    keys_new = jnp.dot(flat_rows, w_k, preferred_element_type=jnp.float32)
    values_new = jnp.dot(flat_rows, w_v, preferred_element_type=jnp.float32)
    square_sums = lax.psum((jnp.sum(queries * queries, -1), jnp.sum(keys_new * keys_new, -1)), "tp")
    full_width = HEADS * HD
    queries = queries * lax.rsqrt(square_sums[0] / full_width + 1e-06)[:, None] * q_gain
    keys_new = keys_new * lax.rsqrt(square_sums[1] / full_width + 1e-06)[:, None] * k_gain
    prefix_len = prefix_cache.shape[1] * lax.axis_size("req")
    length = cache_lens[0]
    positions = (prefix_len + length + jnp.arange(NEW, dtype=jnp.int32)).astype(jnp.float32)
    q_rot = rotate(queries.reshape(NEW, heads_local, HD), positions).astype(jnp.bfloat16)
    k_rot = rotate(keys_new.reshape(NEW, heads_local, HD), positions).astype(jnp.bfloat16)
    v_new = values_new.reshape(NEW, heads_local, HD).astype(jnp.bfloat16)
    appended = jnp.stack([k_rot, v_new], axis=2).reshape(1, NEW, heads_local * 2 * HD)

    shared = chosen.reshape(-1, heads_local, 2, HD)
    cached = cache_rows[0].reshape(-1, heads_local, 2, HD)
    row_ids = jnp.arange(NEW, dtype=jnp.int32)
    columns = jnp.arange(cached.shape[0], dtype=jnp.int32)
    blocks = (
        (shared[:, :, 0], shared[:, :, 1], None),
        (cached[:, :, 0], cached[:, :, 1], (columns < length)[None, :]),
        (k_rot, v_new, row_ids[None, :] <= row_ids[:, None]),
    )
    scores = []
    for keys_block, _, visible in blocks:
        part = jnp.einsum(
            "qhd,khd->hqk", q_rot, keys_block, preferred_element_type=jnp.float32
        ) * HD ** (-0.5)
        if visible is not None:
            part = jnp.where(visible[None], part, -1e30)
        scores.append(part)
    row_peak = functools.reduce(jnp.maximum, [jnp.max(part, -1) for part in scores])
    denominator = 0.0
    weighted = 0.0
    for (_, values_block, visible), part in zip(blocks, scores):
        weights = jnp.exp(part - row_peak[..., None])
        if visible is not None:
            weights = jnp.where(visible[None], weights, 0.0)
        denominator = denominator + jnp.sum(weights, -1)
        weighted = weighted + jnp.einsum(
            "hqk,khd->hqd",
            weights.astype(jnp.bfloat16),
            values_block,
            preferred_element_type=jnp.float32,
        )
    attended = (
        jnp.transpose(weighted / denominator[..., None], (1, 0, 2))
        .reshape(NEW, width_local)
        .astype(jnp.bfloat16)
    )
    partial_out = jnp.dot(attended, w_o, preferred_element_type=jnp.float32)
    blocks_out = partial_out.astype(jnp.bfloat16).reshape(tp_size, -1, partial_out.shape[1])
    mine = jnp.sum(lax.all_to_all(blocks_out, "tp", 0, 0, tiled=True).astype(jnp.float32), 0)
    hidden = (tokens[0].astype(jnp.float32) + rms_scale(mine, out_gain)).astype(jnp.bfloat16)[None]
    return (hidden, appended)


def solution(mesh):
    return jax.shard_map(
        layer,
        mesh=mesh,
        in_specs=(
            P("req", "tp", None),
            P(None, "tp"),
            P(None, "tp"),
            P(None, "tp"),
            P("tp", None),
            P("tp"),
            P("tp"),
            P(),
            P("req"),
            P(),
            P(None, "req", "tp"),
            P("req", None, "tp"),
        ),
        out_specs=(P("req", "tp", None), P("req", None, "tp")),
        check_vma=False,
    )
```

```python
import functools

import jax
import jax.numpy as jnp
from jax import lax
from jax.sharding import PartitionSpec as P

HEADS = 8
HD = 128
NEW = 512


def rotate(values_in, positions):
    half_dim = values_in.shape[-1] // 2
    exponent = jnp.arange(half_dim, dtype=jnp.float32) * (-2.0 / values_in.shape[-1])
    inverse = jnp.power(jnp.float32(500000.0), exponent)
    angles = positions[:, None] * inverse[None, :]
    cosine = jnp.cos(angles)[:, None, :]
    sine_part = jnp.sin(angles)[:, None, :]
    first_half = values_in[..., :half_dim]
    second_half = values_in[..., half_dim:]
    return jnp.concatenate(
        [
            first_half * cosine - second_half * sine_part,
            second_half * cosine + first_half * sine_part,
        ],
        -1,
    )


def rms_scale(values_in, gain_vector):
    mean_sq = jnp.mean(values_in * values_in, axis=-1, keepdims=True)
    return values_in * lax.rsqrt(mean_sq + 1e-06) * gain_vector


def exchange_sum(own, axis, size):
    index = lax.axis_index(axis)
    parts = [own]
    for shift in range(1, size):
        parts.append(lax.ppermute(own, axis, [(i, (i + shift) % size) for i in range(size)]))
    stacked = jnp.stack(parts)
    order = (index - jnp.arange(size)) % size
    by_source = jnp.zeros_like(stacked).at[order].set(stacked)
    return functools.reduce(lambda a, b: a + b, [by_source[i] for i in range(size)])


def layer(
    tokens,
    w_q,
    w_k,
    w_v,
    w_o,
    q_gain,
    k_gain,
    out_gain,
    cache_lens,
    group_ids,
    prefix_cache,
    cache_rows,
):
    heads_local = w_q.shape[1] // HD
    width_local = heads_local * HD
    tp_size = lax.axis_size("tp")
    flat_rows = lax.all_to_all(
        jnp.broadcast_to(tokens, (tp_size,) + tokens.shape[1:]), "tp", 0, 0, tiled=True
    ).reshape(-1, tokens.shape[2])
    outgoing = jnp.take(prefix_cache, group_ids, axis=0)
    chosen = lax.all_to_all(outgoing, "req", 0, 0, tiled=True)
    queries = jnp.dot(flat_rows, w_q, preferred_element_type=jnp.float32)
    keys_new = jnp.dot(flat_rows, w_k, preferred_element_type=jnp.float32)
    values_new = jnp.dot(flat_rows, w_v, preferred_element_type=jnp.float32)
    own_sums = jnp.stack([jnp.sum(queries * queries, -1), jnp.sum(keys_new * keys_new, -1)])
    square_sums = exchange_sum(own_sums, "tp", tp_size)
    full_width = HEADS * HD
    queries = queries * lax.rsqrt(square_sums[0] / full_width + 1e-06)[:, None] * q_gain
    keys_new = keys_new * lax.rsqrt(square_sums[1] / full_width + 1e-06)[:, None] * k_gain
    prefix_len = prefix_cache.shape[1] * lax.axis_size("req")
    length = cache_lens[0]
    positions = (prefix_len + length + jnp.arange(NEW, dtype=jnp.int32)).astype(jnp.float32)
    q_rot = rotate(queries.reshape(NEW, heads_local, HD), positions).astype(jnp.bfloat16)
    k_rot = rotate(keys_new.reshape(NEW, heads_local, HD), positions).astype(jnp.bfloat16)
    v_new = values_new.reshape(NEW, heads_local, HD).astype(jnp.bfloat16)
    appended = jnp.stack([k_rot, v_new], axis=2).reshape(1, NEW, heads_local * 2 * HD)

    shared = chosen.reshape(-1, heads_local, 2, HD)
    cached = cache_rows[0].reshape(-1, heads_local, 2, HD)
    row_ids = jnp.arange(NEW, dtype=jnp.int32)
    columns = jnp.arange(cached.shape[0], dtype=jnp.int32)
    blocks = (
        (shared[:, :, 0], shared[:, :, 1], None),
        (cached[:, :, 0], cached[:, :, 1], (columns < length)[None, :]),
        (k_rot, v_new, row_ids[None, :] <= row_ids[:, None]),
    )
    scores = []
    for keys_block, _, visible in blocks:
        part = jnp.einsum(
            "qhd,khd->hqk", q_rot, keys_block, preferred_element_type=jnp.float32
        ) * HD ** (-0.5)
        if visible is not None:
            part = jnp.where(visible[None], part, -1e30)
        scores.append(part)
    row_peak = functools.reduce(jnp.maximum, [jnp.max(part, -1) for part in scores])
    denominator = 0.0
    weighted = 0.0
    for (_, values_block, visible), part in zip(blocks, scores):
        weights = jnp.exp(part - row_peak[..., None])
        if visible is not None:
            weights = jnp.where(visible[None], weights, 0.0)
        denominator = denominator + jnp.sum(weights, -1)
        weighted = weighted + jnp.einsum(
            "hqk,khd->hqd",
            weights.astype(jnp.bfloat16),
            values_block,
            preferred_element_type=jnp.float32,
        )
    attended = (
        jnp.transpose(weighted / denominator[..., None], (1, 0, 2))
        .reshape(NEW, width_local)
        .astype(jnp.bfloat16)
    )
    partial_out = jnp.dot(attended, w_o, preferred_element_type=jnp.float32)
    blocks_out = partial_out.astype(jnp.bfloat16).reshape(tp_size, -1, partial_out.shape[1])
    mine = jnp.sum(lax.all_to_all(blocks_out, "tp", 0, 0, tiled=True).astype(jnp.float32), 0)
    hidden = (tokens[0].astype(jnp.float32) + rms_scale(mine, out_gain)).astype(jnp.bfloat16)[None]
    return (hidden, appended)


def solution(mesh):
    return jax.shard_map(
        layer,
        mesh=mesh,
        in_specs=(
            P("req", "tp", None),
            P(None, "tp"),
            P(None, "tp"),
            P(None, "tp"),
            P("tp", None),
            P("tp"),
            P("tp"),
            P(),
            P("req"),
            P(),
            P(None, "req", "tp"),
            P("req", None, "tp"),
        ),
        out_specs=(P("req", "tp", None), P("req", None, "tp")),
        check_vma=False,
    )
```

```python
import jax
import jax.numpy as jnp
from jax import lax
from jax.experimental import pallas as pl
from jax.experimental.pallas import tpu as pltpu
from jax.sharding import PartitionSpec as P

HEADS = 8
HD = 128
NEW = 512


def rotate(values_in, positions):
    half_dim = values_in.shape[-1] // 2
    exponent = jnp.arange(half_dim, dtype=jnp.float32) * (-2.0 / values_in.shape[-1])
    inverse = jnp.power(jnp.float32(500000.0), exponent)
    angles = positions[:, None] * inverse[None, :]
    cosine = jnp.cos(angles)[:, None, :]
    sine_part = jnp.sin(angles)[:, None, :]
    first_half = values_in[..., :half_dim]
    second_half = values_in[..., half_dim:]
    return jnp.concatenate(
        [
            first_half * cosine - second_half * sine_part,
            second_half * cosine + first_half * sine_part,
        ],
        -1,
    )


def rms_scale(values_in, gain_vector):
    mean_sq = jnp.mean(values_in * values_in, axis=-1, keepdims=True)
    return values_in * lax.rsqrt(mean_sq + 1e-06) * gain_vector


QUERY_BLOCK = 128
KEY_BLOCK = 512


def attend_kernel(len_ref, q_ref, pre_ref, cache_ref, nk_ref, nv_ref, out_ref, score_ref):
    block = pl.program_id(0)
    length = len_ref[0]
    queries = q_ref[...]
    scale = HD ** (-0.5)
    prefix_chunks = pre_ref.shape[0] // KEY_BLOCK
    cache_chunks = cache_ref.shape[0] // KEY_BLOCK
    row_ids = block * QUERY_BLOCK + lax.broadcasted_iota(jnp.int32, (QUERY_BLOCK, KEY_BLOCK), 0)
    col_ids = lax.broadcasted_iota(jnp.int32, (QUERY_BLOCK, KEY_BLOCK), 1)

    def keys_of(chunk):
        if chunk < prefix_chunks:
            return pre_ref[pl.ds(chunk * KEY_BLOCK, KEY_BLOCK), pl.ds(0, HD)]
        if chunk < prefix_chunks + cache_chunks:
            start = (chunk - prefix_chunks) * KEY_BLOCK
            return cache_ref[pl.ds(start, KEY_BLOCK), pl.ds(0, HD)]
        return nk_ref[...]

    def values_of(chunk):
        if chunk < prefix_chunks:
            return pre_ref[pl.ds(chunk * KEY_BLOCK, KEY_BLOCK), pl.ds(HD, HD)]
        if chunk < prefix_chunks + cache_chunks:
            start = (chunk - prefix_chunks) * KEY_BLOCK
            return cache_ref[pl.ds(start, KEY_BLOCK), pl.ds(HD, HD)]
        return nv_ref[...]

    def visible_of(chunk):
        if chunk < prefix_chunks:
            return None
        if chunk < prefix_chunks + cache_chunks:
            return col_ids + (chunk - prefix_chunks) * KEY_BLOCK < length
        return col_ids <= row_ids

    chunks = prefix_chunks + cache_chunks + 1
    row_peak = None
    for chunk in range(chunks):
        part = lax.dot_general(
            queries, keys_of(chunk), (((1,), (1,)), ((), ())),
            preferred_element_type=jnp.float32,
        ) * scale
        visible = visible_of(chunk)
        if visible is not None:
            part = jnp.where(visible, part, -1e30)
        score_ref[:, pl.ds(chunk * KEY_BLOCK, KEY_BLOCK)] = part
        peak = jnp.max(part, -1, keepdims=True)
        row_peak = peak if row_peak is None else jnp.maximum(row_peak, peak)
    denominator = jnp.zeros((QUERY_BLOCK, 1), jnp.float32)
    weighted = jnp.zeros((QUERY_BLOCK, HD), jnp.float32)
    for chunk in range(chunks):
        weights = jnp.exp(score_ref[:, pl.ds(chunk * KEY_BLOCK, KEY_BLOCK)] - row_peak)
        visible = visible_of(chunk)
        if visible is not None:
            weights = jnp.where(visible, weights, 0.0)
        denominator = denominator + jnp.sum(weights, -1, keepdims=True)
        weighted = weighted + jnp.dot(
            weights.astype(jnp.bfloat16), values_of(chunk), preferred_element_type=jnp.float32
        )
    out_ref[...] = (weighted / denominator).astype(out_ref.dtype)


def attend(cache_lens, queries, prefix_pairs, cache_pairs, keys_new, values_new):
    new_rows = queries.shape[0]
    whole = lambda block, lens: (0, 0)
    rows = lambda block, lens: (block, 0)
    chunks = (prefix_pairs.shape[0] + cache_pairs.shape[0]) // KEY_BLOCK + 1
    return pl.pallas_call(
        attend_kernel,
        grid_spec=pltpu.PrefetchScalarGridSpec(
            num_scalar_prefetch=1,
            grid=(new_rows // QUERY_BLOCK,),
            in_specs=[
                pl.BlockSpec((QUERY_BLOCK, HD), rows),
                pl.BlockSpec(prefix_pairs.shape, whole),
                pl.BlockSpec(cache_pairs.shape, whole),
                pl.BlockSpec(keys_new.shape, whole),
                pl.BlockSpec(values_new.shape, whole),
            ],
            out_specs=pl.BlockSpec((QUERY_BLOCK, HD), rows),
            scratch_shapes=[pltpu.VMEM((QUERY_BLOCK, chunks * KEY_BLOCK), jnp.float32)],
        ),
        out_shape=jax.ShapeDtypeStruct((new_rows, HD), jnp.bfloat16),
        compiler_params=pltpu.CompilerParams(dimension_semantics=("arbitrary",)),
    )(cache_lens, queries, prefix_pairs, cache_pairs, keys_new, values_new)


def layer(
    tokens,
    w_q,
    w_k,
    w_v,
    w_o,
    q_gain,
    k_gain,
    out_gain,
    cache_lens,
    group_ids,
    prefix_cache,
    cache_rows,
):
    heads_local = w_q.shape[1] // HD
    tp_size = lax.axis_size("tp")
    flat_rows = lax.all_to_all(
        jnp.broadcast_to(tokens, (tp_size,) + tokens.shape[1:]), "tp", 0, 0, tiled=True
    ).reshape(-1, tokens.shape[2])
    outgoing = jnp.take(prefix_cache, group_ids, axis=0)
    chosen = lax.all_to_all(outgoing, "req", 0, 0, tiled=True)
    queries = jnp.dot(flat_rows, w_q, preferred_element_type=jnp.float32)
    keys_new = jnp.dot(flat_rows, w_k, preferred_element_type=jnp.float32)
    values_new = jnp.dot(flat_rows, w_v, preferred_element_type=jnp.float32)
    square_sums = lax.psum((jnp.sum(queries * queries, -1), jnp.sum(keys_new * keys_new, -1)), "tp")
    full_width = HEADS * HD
    queries = queries * lax.rsqrt(square_sums[0] / full_width + 1e-06)[:, None] * q_gain
    keys_new = keys_new * lax.rsqrt(square_sums[1] / full_width + 1e-06)[:, None] * k_gain
    prefix_len = prefix_cache.shape[1] * lax.axis_size("req")
    length = cache_lens[0]
    positions = (prefix_len + length + jnp.arange(NEW, dtype=jnp.int32)).astype(jnp.float32)
    q_rot = rotate(queries.reshape(NEW, heads_local, HD), positions).astype(jnp.bfloat16)
    k_rot = rotate(keys_new.reshape(NEW, heads_local, HD), positions).astype(jnp.bfloat16)
    v_new = values_new.reshape(NEW, heads_local, HD).astype(jnp.bfloat16)
    appended = jnp.stack([k_rot, v_new], axis=2).reshape(1, NEW, heads_local * 2 * HD)

    shared = chosen.reshape(-1, heads_local * 2 * HD)
    cached = cache_rows[0]
    heads_out = []
    for head in range(heads_local):
        pair = slice(head * 2 * HD, (head + 1) * 2 * HD)
        heads_out.append(
            attend(
                cache_lens,
                q_rot[:, head],
                shared[:, pair],
                cached[:, pair],
                k_rot[:, head],
                v_new[:, head],
            )
        )
    attended = jnp.concatenate(heads_out, -1)
    partial_out = jnp.dot(attended, w_o, preferred_element_type=jnp.float32)
    blocks_out = partial_out.astype(jnp.bfloat16).reshape(tp_size, -1, partial_out.shape[1])
    mine = jnp.sum(lax.all_to_all(blocks_out, "tp", 0, 0, tiled=True).astype(jnp.float32), 0)
    hidden = (tokens[0].astype(jnp.float32) + rms_scale(mine, out_gain)).astype(jnp.bfloat16)[None]
    return (hidden, appended)


def solution(mesh):
    return jax.shard_map(
        layer,
        mesh=mesh,
        in_specs=(
            P("req", "tp", None),
            P(None, "tp"),
            P(None, "tp"),
            P(None, "tp"),
            P("tp", None),
            P("tp"),
            P("tp"),
            P(),
            P("req"),
            P(),
            P(None, "req", "tp"),
            P("req", None, "tp"),
        ),
        out_specs=(P("req", "tp", None), P("req", None, "tp")),
        check_vma=False,
    )
```

```python
import jax
import jax.numpy as jnp
from jax import lax
from jax.experimental import pallas as pl
from jax.experimental.pallas import tpu as pltpu
from jax.sharding import Mesh, PartitionSpec as P

HEADS = 8
HD = 128
NEW = 512


def rotate(values_in, positions):
    half_dim = values_in.shape[-1] // 2
    exponent = jnp.arange(half_dim, dtype=jnp.float32) * (-2.0 / values_in.shape[-1])
    inverse = jnp.power(jnp.float32(500000.0), exponent)
    angles = positions[:, None] * inverse[None, :]
    cosine = jnp.cos(angles)[:, None, :]
    sine_part = jnp.sin(angles)[:, None, :]
    first_half = values_in[..., :half_dim]
    second_half = values_in[..., half_dim:]
    return jnp.concatenate(
        [
            first_half * cosine - second_half * sine_part,
            second_half * cosine + first_half * sine_part,
        ],
        -1,
    )


def rms_scale(values_in, gain_vector):
    mean_sq = jnp.mean(values_in * values_in, axis=-1, keepdims=True)
    return values_in * lax.rsqrt(mean_sq + 1e-06) * gain_vector


QUERY_BLOCK = 128
KEY_BLOCK = 512


def attend_kernel(len_ref, q_ref, pre_ref, cache_ref, nk_ref, nv_ref, out_ref, score_ref):
    block = pl.program_id(0)
    length = len_ref[0]
    queries = q_ref[...]
    scale = HD ** (-0.5)
    prefix_chunks = pre_ref.shape[0] // KEY_BLOCK
    cache_chunks = cache_ref.shape[0] // KEY_BLOCK
    row_ids = block * QUERY_BLOCK + lax.broadcasted_iota(jnp.int32, (QUERY_BLOCK, KEY_BLOCK), 0)
    col_ids = lax.broadcasted_iota(jnp.int32, (QUERY_BLOCK, KEY_BLOCK), 1)

    def keys_of(chunk):
        if chunk < prefix_chunks:
            return pre_ref[pl.ds(chunk * KEY_BLOCK, KEY_BLOCK), pl.ds(0, HD)]
        if chunk < prefix_chunks + cache_chunks:
            start = (chunk - prefix_chunks) * KEY_BLOCK
            return cache_ref[pl.ds(start, KEY_BLOCK), pl.ds(0, HD)]
        return nk_ref[...]

    def values_of(chunk):
        if chunk < prefix_chunks:
            return pre_ref[pl.ds(chunk * KEY_BLOCK, KEY_BLOCK), pl.ds(HD, HD)]
        if chunk < prefix_chunks + cache_chunks:
            start = (chunk - prefix_chunks) * KEY_BLOCK
            return cache_ref[pl.ds(start, KEY_BLOCK), pl.ds(HD, HD)]
        return nv_ref[...]

    def visible_of(chunk):
        if chunk < prefix_chunks:
            return None
        if chunk < prefix_chunks + cache_chunks:
            return col_ids + (chunk - prefix_chunks) * KEY_BLOCK < length
        return col_ids <= row_ids

    chunks = prefix_chunks + cache_chunks + 1
    row_peak = None
    for chunk in range(chunks):
        part = lax.dot_general(
            queries, keys_of(chunk), (((1,), (1,)), ((), ())),
            preferred_element_type=jnp.float32,
        ) * scale
        visible = visible_of(chunk)
        if visible is not None:
            part = jnp.where(visible, part, -1e30)
        score_ref[:, pl.ds(chunk * KEY_BLOCK, KEY_BLOCK)] = part
        peak = jnp.max(part, -1, keepdims=True)
        row_peak = peak if row_peak is None else jnp.maximum(row_peak, peak)
    denominator = jnp.zeros((QUERY_BLOCK, 1), jnp.float32)
    weighted = jnp.zeros((QUERY_BLOCK, HD), jnp.float32)
    for chunk in range(chunks):
        weights = jnp.exp(score_ref[:, pl.ds(chunk * KEY_BLOCK, KEY_BLOCK)] - row_peak)
        visible = visible_of(chunk)
        if visible is not None:
            weights = jnp.where(visible, weights, 0.0)
        denominator = denominator + jnp.sum(weights, -1, keepdims=True)
        weighted = weighted + jnp.dot(
            weights.astype(jnp.bfloat16), values_of(chunk), preferred_element_type=jnp.float32
        )
    out_ref[...] = (weighted / denominator).astype(out_ref.dtype)


def attend(cache_lens, queries, prefix_pairs, cache_pairs, keys_new, values_new):
    new_rows = queries.shape[0]
    whole = lambda block, lens: (0, 0)
    rows = lambda block, lens: (block, 0)
    chunks = (prefix_pairs.shape[0] + cache_pairs.shape[0]) // KEY_BLOCK + 1
    return pl.pallas_call(
        attend_kernel,
        grid_spec=pltpu.PrefetchScalarGridSpec(
            num_scalar_prefetch=1,
            grid=(new_rows // QUERY_BLOCK,),
            in_specs=[
                pl.BlockSpec((QUERY_BLOCK, HD), rows),
                pl.BlockSpec(prefix_pairs.shape, whole),
                pl.BlockSpec(cache_pairs.shape, whole),
                pl.BlockSpec(keys_new.shape, whole),
                pl.BlockSpec(values_new.shape, whole),
            ],
            out_specs=pl.BlockSpec((QUERY_BLOCK, HD), rows),
            scratch_shapes=[pltpu.VMEM((QUERY_BLOCK, chunks * KEY_BLOCK), jnp.float32)],
        ),
        out_shape=jax.ShapeDtypeStruct((new_rows, HD), jnp.bfloat16),
        compiler_params=pltpu.CompilerParams(dimension_semantics=("arbitrary",)),
    )(cache_lens, queries, prefix_pairs, cache_pairs, keys_new, values_new)


REQ_AXES = ("req_hi", "req_mid", "req_lo")


def exchange_prefix(prefix_cache, group_ids):
    hi, mid, lo = (lax.axis_size(name) for name in REQ_AXES)
    rows, width = prefix_cache.shape[1:]
    dest = (
        jnp.arange(hi)[:, None, None] * (mid * lo)
        + jnp.arange(lo)[None, :, None]
        + jnp.arange(mid)[None, None, :] * lo
    ).reshape(-1)
    outgoing = jnp.take(prefix_cache, jnp.take(group_ids, dest), axis=0)
    first = lax.all_to_all(outgoing, ("req_hi", "req_lo"), 0, 0, tiled=True)
    first = first.reshape(hi * lo, mid, rows, width).transpose(1, 0, 2, 3)
    second = lax.all_to_all(first.reshape(-1, rows, width), "req_mid", 0, 0, tiled=True)
    second = second.reshape(mid, hi, lo, rows, width).transpose(1, 0, 2, 3, 4)
    return second.reshape(-1, width)


def layer(
    tokens,
    w_q,
    w_k,
    w_v,
    w_o,
    q_gain,
    k_gain,
    out_gain,
    cache_lens,
    group_ids,
    prefix_cache,
    cache_rows,
):
    heads_local = w_q.shape[1] // HD
    tp_size = lax.axis_size("tp")
    flat_rows = lax.all_to_all(
        jnp.broadcast_to(tokens, (tp_size,) + tokens.shape[1:]), "tp", 0, 0, tiled=True
    ).reshape(-1, tokens.shape[2])
    chosen = exchange_prefix(prefix_cache, group_ids)
    queries = jnp.dot(flat_rows, w_q, preferred_element_type=jnp.float32)
    keys_new = jnp.dot(flat_rows, w_k, preferred_element_type=jnp.float32)
    values_new = jnp.dot(flat_rows, w_v, preferred_element_type=jnp.float32)
    square_sums = lax.psum((jnp.sum(queries * queries, -1), jnp.sum(keys_new * keys_new, -1)), "tp")
    full_width = HEADS * HD
    queries = queries * lax.rsqrt(square_sums[0] / full_width + 1e-06)[:, None] * q_gain
    keys_new = keys_new * lax.rsqrt(square_sums[1] / full_width + 1e-06)[:, None] * k_gain
    prefix_len = prefix_cache.shape[1] * lax.axis_size(REQ_AXES)
    length = cache_lens[0]
    positions = (prefix_len + length + jnp.arange(NEW, dtype=jnp.int32)).astype(jnp.float32)
    q_rot = rotate(queries.reshape(NEW, heads_local, HD), positions).astype(jnp.bfloat16)
    k_rot = rotate(keys_new.reshape(NEW, heads_local, HD), positions).astype(jnp.bfloat16)
    v_new = values_new.reshape(NEW, heads_local, HD).astype(jnp.bfloat16)
    appended = jnp.stack([k_rot, v_new], axis=2).reshape(1, NEW, heads_local * 2 * HD)

    shared = chosen.reshape(-1, heads_local * 2 * HD)
    cached = cache_rows[0]
    heads_out = []
    for head in range(heads_local):
        pair = slice(head * 2 * HD, (head + 1) * 2 * HD)
        heads_out.append(
            attend(
                cache_lens,
                q_rot[:, head],
                shared[:, pair],
                cached[:, pair],
                k_rot[:, head],
                v_new[:, head],
            )
        )
    attended = jnp.concatenate(heads_out, -1)
    partial_out = jnp.dot(attended, w_o, preferred_element_type=jnp.float32)
    blocks_out = partial_out.astype(jnp.bfloat16).reshape(tp_size, -1, partial_out.shape[1])
    mine = jnp.sum(lax.all_to_all(blocks_out, "tp", 0, 0, tiled=True).astype(jnp.float32), 0)
    hidden = (tokens[0].astype(jnp.float32) + rms_scale(mine, out_gain)).astype(jnp.bfloat16)[None]
    return (hidden, appended)


def solution(mesh):
    req_size = mesh.shape["req"]
    lo = 2 if req_size % 2 == 0 else 1
    mid = 16 if (req_size // lo) % 16 == 0 else req_size // lo
    hi = req_size // (lo * mid)
    split_mesh = Mesh(
        mesh.devices.reshape(hi, mid, lo, mesh.shape["tp"]), REQ_AXES + ("tp",)
    )
    req = REQ_AXES
    return jax.shard_map(
        layer,
        mesh=split_mesh,
        in_specs=(
            P(req, "tp", None),
            P(None, "tp"),
            P(None, "tp"),
            P(None, "tp"),
            P("tp", None),
            P("tp"),
            P("tp"),
            P(),
            P(req),
            P(),
            P(None, req, "tp"),
            P(req, None, "tp"),
        ),
        out_specs=(P(req, "tp", None), P(req, None, "tp")),
        check_vma=False,
    )
```

```python
import jax
import jax.numpy as jnp
from jax import lax
from jax.experimental import pallas as pl
from jax.experimental.pallas import tpu as pltpu
from jax.sharding import PartitionSpec as P

HEADS = 8
HD = 128
NEW = 512


def rotate(values_in, positions):
    half_dim = values_in.shape[-1] // 2
    exponent = jnp.arange(half_dim, dtype=jnp.float32) * (-2.0 / values_in.shape[-1])
    inverse = jnp.power(jnp.float32(500000.0), exponent)
    angles = positions[:, None] * inverse[None, :]
    cosine = jnp.cos(angles)[:, None, :]
    sine_part = jnp.sin(angles)[:, None, :]
    first_half = values_in[..., :half_dim]
    second_half = values_in[..., half_dim:]
    return jnp.concatenate(
        [
            first_half * cosine - second_half * sine_part,
            second_half * cosine + first_half * sine_part,
        ],
        -1,
    )


def rms_scale(values_in, gain_vector):
    mean_sq = jnp.mean(values_in * values_in, axis=-1, keepdims=True)
    return values_in * lax.rsqrt(mean_sq + 1e-06) * gain_vector


QUERY_BLOCK = 128
KEY_BLOCK = 512


def attend_kernel(len_ref, q_ref, pre_ref, cache_ref, nk_ref, nv_ref, wo_ref, out_ref, score_ref):
    block = pl.program_id(0)
    length = len_ref[0]
    queries = q_ref[...]
    scale = HD ** (-0.5)
    prefix_chunks = pre_ref.shape[0] // KEY_BLOCK
    cache_chunks = cache_ref.shape[0] // KEY_BLOCK
    row_ids = block * QUERY_BLOCK + lax.broadcasted_iota(jnp.int32, (QUERY_BLOCK, KEY_BLOCK), 0)
    col_ids = lax.broadcasted_iota(jnp.int32, (QUERY_BLOCK, KEY_BLOCK), 1)

    def keys_of(chunk):
        if chunk < prefix_chunks:
            return pre_ref[pl.ds(chunk * KEY_BLOCK, KEY_BLOCK), pl.ds(0, HD)]
        if chunk < prefix_chunks + cache_chunks:
            start = (chunk - prefix_chunks) * KEY_BLOCK
            return cache_ref[pl.ds(start, KEY_BLOCK), pl.ds(0, HD)]
        return nk_ref[...]

    def values_of(chunk):
        if chunk < prefix_chunks:
            return pre_ref[pl.ds(chunk * KEY_BLOCK, KEY_BLOCK), pl.ds(HD, HD)]
        if chunk < prefix_chunks + cache_chunks:
            start = (chunk - prefix_chunks) * KEY_BLOCK
            return cache_ref[pl.ds(start, KEY_BLOCK), pl.ds(HD, HD)]
        return nv_ref[...]

    def visible_of(chunk):
        if chunk < prefix_chunks:
            return None
        if chunk == prefix_chunks:
            return None
        if chunk < prefix_chunks + cache_chunks:
            return col_ids + (chunk - prefix_chunks) * KEY_BLOCK < length
        return col_ids <= row_ids

    chunks = prefix_chunks + cache_chunks + 1
    row_peak = None
    for chunk in range(chunks):
        part = lax.dot_general(
            queries, keys_of(chunk), (((1,), (1,)), ((), ())),
            preferred_element_type=jnp.float32,
        ) * scale
        visible = visible_of(chunk)
        if visible is not None:
            part = jnp.where(visible, part, -1e30)
        score_ref[:, pl.ds(chunk * KEY_BLOCK, KEY_BLOCK)] = part
        peak = jnp.max(part, -1, keepdims=True)
        row_peak = peak if row_peak is None else jnp.maximum(row_peak, peak)
    denominator = jnp.zeros((QUERY_BLOCK, 1), jnp.float32)
    weighted = jnp.zeros((QUERY_BLOCK, HD), jnp.float32)
    for chunk in range(chunks):
        weights = jnp.exp(score_ref[:, pl.ds(chunk * KEY_BLOCK, KEY_BLOCK)] - row_peak)
        visible = visible_of(chunk)
        if visible is not None:
            weights = jnp.where(visible, weights, 0.0)
        denominator = denominator + jnp.sum(weights, -1, keepdims=True)
        weighted = weighted + jnp.dot(
            weights.astype(jnp.bfloat16), values_of(chunk), preferred_element_type=jnp.float32
        )
    attended = (weighted / denominator).astype(jnp.bfloat16)
    out_ref[...] = jnp.dot(
        attended, wo_ref[...], preferred_element_type=jnp.float32
    ).astype(out_ref.dtype)


def attend(cache_lens, queries, prefix_pairs, cache_pairs, keys_new, values_new, w_out):
    new_rows = queries.shape[0]
    whole = lambda block, lens: (0, 0)
    rows = lambda block, lens: (block, 0)
    chunks = (prefix_pairs.shape[0] + cache_pairs.shape[0]) // KEY_BLOCK + 1
    return pl.pallas_call(
        attend_kernel,
        grid_spec=pltpu.PrefetchScalarGridSpec(
            num_scalar_prefetch=1,
            grid=(new_rows // QUERY_BLOCK,),
            in_specs=[
                pl.BlockSpec((QUERY_BLOCK, HD), rows),
                pl.BlockSpec(prefix_pairs.shape, whole),
                pl.BlockSpec(cache_pairs.shape, whole),
                pl.BlockSpec(keys_new.shape, whole),
                pl.BlockSpec(values_new.shape, whole),
                pl.BlockSpec(w_out.shape, whole),
            ],
            out_specs=pl.BlockSpec((QUERY_BLOCK, w_out.shape[1]), rows),
            scratch_shapes=[pltpu.VMEM((QUERY_BLOCK, chunks * KEY_BLOCK), jnp.float32)],
        ),
        out_shape=jax.ShapeDtypeStruct((new_rows, w_out.shape[1]), jnp.bfloat16),
        compiler_params=pltpu.CompilerParams(dimension_semantics=("arbitrary",)),
    )(cache_lens, queries, prefix_pairs, cache_pairs, keys_new, values_new, w_out)


def layer(
    tokens,
    w_q,
    w_k,
    w_v,
    w_o,
    q_gain,
    k_gain,
    out_gain,
    cache_lens,
    group_ids,
    prefix_cache,
    cache_rows,
):
    heads_local = w_q.shape[1] // HD
    tp_size = lax.axis_size("tp")
    flat_rows = lax.all_to_all(
        jnp.broadcast_to(tokens, (tp_size,) + tokens.shape[1:]), "tp", 0, 0, tiled=True
    ).reshape(-1, tokens.shape[2])
    outgoing = jnp.take(prefix_cache, group_ids, axis=0)
    chosen = lax.all_to_all(outgoing, "req", 0, 0, tiled=True)
    queries = jnp.dot(flat_rows, w_q, preferred_element_type=jnp.float32)
    keys_new = jnp.dot(flat_rows, w_k, preferred_element_type=jnp.float32)
    values_new = jnp.dot(flat_rows, w_v, preferred_element_type=jnp.float32)
    square_sums = lax.psum((jnp.sum(queries * queries, -1), jnp.sum(keys_new * keys_new, -1)), "tp")
    full_width = HEADS * HD
    queries = queries * lax.rsqrt(square_sums[0] / full_width + 1e-06)[:, None] * q_gain
    keys_new = keys_new * lax.rsqrt(square_sums[1] / full_width + 1e-06)[:, None] * k_gain
    prefix_len = prefix_cache.shape[1] * lax.axis_size("req")
    length = cache_lens[0]
    positions = (prefix_len + length + jnp.arange(NEW, dtype=jnp.int32)).astype(jnp.float32)
    q_rot = rotate(queries.reshape(NEW, heads_local, HD), positions).astype(jnp.bfloat16)
    k_rot = rotate(keys_new.reshape(NEW, heads_local, HD), positions).astype(jnp.bfloat16)
    v_new = values_new.reshape(NEW, heads_local, HD).astype(jnp.bfloat16)
    appended = jnp.stack([k_rot, v_new], axis=2).reshape(1, NEW, heads_local * 2 * HD)

    shared = chosen.reshape(-1, heads_local * 2 * HD)
    cached = cache_rows[0]
    partial_sum = None
    for head in range(heads_local):
        pair = slice(head * 2 * HD, (head + 1) * 2 * HD)
        partial = attend(
            cache_lens,
            q_rot[:, head],
            shared[:, pair],
            cached[:, pair],
            k_rot[:, head],
            v_new[:, head],
            w_o[head * HD : (head + 1) * HD],
        )
        partial = partial if heads_local == 1 else partial.astype(jnp.float32)
        partial_sum = partial if partial_sum is None else partial_sum + partial
    partial_out = partial_sum.astype(jnp.bfloat16)
    blocks_out = partial_out.astype(jnp.bfloat16).reshape(tp_size, -1, partial_out.shape[1])
    mine = jnp.sum(lax.all_to_all(blocks_out, "tp", 0, 0, tiled=True).astype(jnp.float32), 0)
    hidden = (tokens[0].astype(jnp.float32) + rms_scale(mine, out_gain)).astype(jnp.bfloat16)[None]
    return (hidden, appended)


def solution(mesh):
    return jax.shard_map(
        layer,
        mesh=mesh,
        in_specs=(
            P("req", "tp", None),
            P(None, "tp"),
            P(None, "tp"),
            P(None, "tp"),
            P("tp", None),
            P("tp"),
            P("tp"),
            P(),
            P("req"),
            P(),
            P(None, "req", "tp"),
            P("req", None, "tp"),
        ),
        out_specs=(P("req", "tp", None), P("req", None, "tp")),
        check_vma=False,
    )
```

```python
import jax
import jax.numpy as jnp
from jax import lax
from jax.experimental import pallas as pl
from jax.experimental.pallas import tpu as pltpu
from jax.sharding import PartitionSpec as P

HEADS = 8
HD = 128
NEW = 512


def rotate(values_in, positions):
    half_dim = values_in.shape[-1] // 2
    exponent = jnp.arange(half_dim, dtype=jnp.float32) * (-2.0 / values_in.shape[-1])
    inverse = jnp.power(jnp.float32(500000.0), exponent)
    angles = positions[:, None] * inverse[None, :]
    cosine = jnp.cos(angles)[:, None, :]
    sine_part = jnp.sin(angles)[:, None, :]
    first_half = values_in[..., :half_dim]
    second_half = values_in[..., half_dim:]
    return jnp.concatenate(
        [
            first_half * cosine - second_half * sine_part,
            second_half * cosine + first_half * sine_part,
        ],
        -1,
    )


def rms_scale(values_in, gain_vector):
    mean_sq = jnp.mean(values_in * values_in, axis=-1, keepdims=True)
    return values_in * lax.rsqrt(mean_sq + 1e-06) * gain_vector


QUERY_BLOCK = 128
KEY_BLOCK = 512


def attend_kernel(len_ref, q_ref, pre_ref, cache_ref, nk_ref, nv_ref, wo_ref, out_ref, score_ref):
    block = pl.program_id(0)
    length = len_ref[0]
    queries = q_ref[...]
    scale = HD ** (-0.5)
    prefix_chunks = pre_ref.shape[0] // KEY_BLOCK
    cache_chunks = cache_ref.shape[0] // KEY_BLOCK
    row_ids = block * QUERY_BLOCK + lax.broadcasted_iota(jnp.int32, (QUERY_BLOCK, KEY_BLOCK), 0)
    col_ids = lax.broadcasted_iota(jnp.int32, (QUERY_BLOCK, KEY_BLOCK), 1)

    def keys_of(chunk):
        if chunk < prefix_chunks:
            return pre_ref[pl.ds(chunk * KEY_BLOCK, KEY_BLOCK), pl.ds(0, HD)]
        if chunk < prefix_chunks + cache_chunks:
            start = (chunk - prefix_chunks) * KEY_BLOCK
            return cache_ref[pl.ds(start, KEY_BLOCK), pl.ds(0, HD)]
        return nk_ref[...]

    def values_of(chunk):
        if chunk < prefix_chunks:
            return pre_ref[pl.ds(chunk * KEY_BLOCK, KEY_BLOCK), pl.ds(HD, HD)]
        if chunk < prefix_chunks + cache_chunks:
            start = (chunk - prefix_chunks) * KEY_BLOCK
            return cache_ref[pl.ds(start, KEY_BLOCK), pl.ds(HD, HD)]
        return nv_ref[...]

    def visible_of(chunk):
        if chunk < prefix_chunks:
            return None
        if chunk == prefix_chunks:
            return None
        if chunk < prefix_chunks + cache_chunks:
            return col_ids + (chunk - prefix_chunks) * KEY_BLOCK < length
        return col_ids <= row_ids

    chunks = prefix_chunks + cache_chunks + 1
    row_peak = None
    for chunk in range(chunks):
        part = lax.dot_general(
            queries, keys_of(chunk), (((1,), (1,)), ((), ())),
            preferred_element_type=jnp.float32,
        ) * scale
        visible = visible_of(chunk)
        if visible is not None and prefix_chunks < chunk < prefix_chunks + cache_chunks:
            end = (chunk - prefix_chunks + 1) * KEY_BLOCK
            part = lax.cond(
                end <= length,
                lambda p: p,
                lambda p: jnp.where(visible, p, -1e30),
                part,
            )
        elif visible is not None:
            part = jnp.where(visible, part, -1e30)
        score_ref[:, pl.ds(chunk * KEY_BLOCK, KEY_BLOCK)] = part
        peak = jnp.max(part, -1, keepdims=True)
        row_peak = peak if row_peak is None else jnp.maximum(row_peak, peak)
    denominator = jnp.zeros((QUERY_BLOCK, 1), jnp.float32)
    weighted = jnp.zeros((QUERY_BLOCK, HD), jnp.float32)
    for chunk in range(chunks):
        weights = jnp.exp(score_ref[:, pl.ds(chunk * KEY_BLOCK, KEY_BLOCK)] - row_peak)
        denominator = denominator + jnp.sum(weights, -1, keepdims=True)
        weighted = weighted + jnp.dot(
            weights.astype(jnp.bfloat16), values_of(chunk), preferred_element_type=jnp.float32
        )
    attended = (weighted / denominator).astype(jnp.bfloat16)
    out_ref[...] = jnp.dot(
        attended, wo_ref[...], preferred_element_type=jnp.float32
    ).astype(out_ref.dtype)


def attend(cache_lens, queries, prefix_pairs, cache_pairs, keys_new, values_new, w_out):
    new_rows = queries.shape[0]
    whole = lambda block, lens: (0, 0)
    rows = lambda block, lens: (block, 0)
    chunks = (prefix_pairs.shape[0] + cache_pairs.shape[0]) // KEY_BLOCK + 1
    return pl.pallas_call(
        attend_kernel,
        grid_spec=pltpu.PrefetchScalarGridSpec(
            num_scalar_prefetch=1,
            grid=(new_rows // QUERY_BLOCK,),
            in_specs=[
                pl.BlockSpec((QUERY_BLOCK, HD), rows),
                pl.BlockSpec(prefix_pairs.shape, whole),
                pl.BlockSpec(cache_pairs.shape, whole),
                pl.BlockSpec(keys_new.shape, whole),
                pl.BlockSpec(values_new.shape, whole),
                pl.BlockSpec(w_out.shape, whole),
            ],
            out_specs=pl.BlockSpec((QUERY_BLOCK, w_out.shape[1]), rows),
            scratch_shapes=[pltpu.VMEM((QUERY_BLOCK, chunks * KEY_BLOCK), jnp.float32)],
        ),
        out_shape=jax.ShapeDtypeStruct((new_rows, w_out.shape[1]), jnp.bfloat16),
        compiler_params=pltpu.CompilerParams(dimension_semantics=("arbitrary",)),
    )(cache_lens, queries, prefix_pairs, cache_pairs, keys_new, values_new, w_out)


def layer(
    tokens,
    w_q,
    w_k,
    w_v,
    w_o,
    q_gain,
    k_gain,
    out_gain,
    cache_lens,
    group_ids,
    prefix_cache,
    cache_rows,
):
    heads_local = w_q.shape[1] // HD
    tp_size = lax.axis_size("tp")
    flat_rows = lax.all_to_all(
        jnp.broadcast_to(tokens, (tp_size,) + tokens.shape[1:]), "tp", 0, 0, tiled=True
    ).reshape(-1, tokens.shape[2])
    outgoing = jnp.take(prefix_cache, group_ids, axis=0)
    chosen = lax.all_to_all(outgoing, "req", 0, 0, tiled=True)
    queries = jnp.dot(flat_rows, w_q, preferred_element_type=jnp.float32)
    keys_new = jnp.dot(flat_rows, w_k, preferred_element_type=jnp.float32)
    values_new = jnp.dot(flat_rows, w_v, preferred_element_type=jnp.float32)
    square_sums = lax.psum((jnp.sum(queries * queries, -1), jnp.sum(keys_new * keys_new, -1)), "tp")
    full_width = HEADS * HD
    queries = queries * lax.rsqrt(square_sums[0] / full_width + 1e-06)[:, None] * q_gain
    keys_new = keys_new * lax.rsqrt(square_sums[1] / full_width + 1e-06)[:, None] * k_gain
    prefix_len = prefix_cache.shape[1] * lax.axis_size("req")
    length = cache_lens[0]
    positions = (prefix_len + length + jnp.arange(NEW, dtype=jnp.int32)).astype(jnp.float32)
    q_rot = rotate(queries.reshape(NEW, heads_local, HD), positions).astype(jnp.bfloat16)
    k_rot = rotate(keys_new.reshape(NEW, heads_local, HD), positions).astype(jnp.bfloat16)
    v_new = values_new.reshape(NEW, heads_local, HD).astype(jnp.bfloat16)
    appended = jnp.stack([k_rot, v_new], axis=2).reshape(1, NEW, heads_local * 2 * HD)

    shared = chosen.reshape(-1, heads_local * 2 * HD)
    cached = cache_rows[0]
    partial_sum = None
    for head in range(heads_local):
        pair = slice(head * 2 * HD, (head + 1) * 2 * HD)
        partial = attend(
            cache_lens,
            q_rot[:, head],
            shared[:, pair],
            cached[:, pair],
            k_rot[:, head],
            v_new[:, head],
            w_o[head * HD : (head + 1) * HD],
        )
        partial = partial if heads_local == 1 else partial.astype(jnp.float32)
        partial_sum = partial if partial_sum is None else partial_sum + partial
    partial_out = partial_sum.astype(jnp.bfloat16)
    blocks_out = partial_out.astype(jnp.bfloat16).reshape(tp_size, -1, partial_out.shape[1])
    mine = jnp.sum(lax.all_to_all(blocks_out, "tp", 0, 0, tiled=True).astype(jnp.float32), 0)
    hidden = (tokens[0].astype(jnp.float32) + rms_scale(mine, out_gain)).astype(jnp.bfloat16)[None]
    return (hidden, appended)


def solution(mesh):
    return jax.shard_map(
        layer,
        mesh=mesh,
        in_specs=(
            P("req", "tp", None),
            P(None, "tp"),
            P(None, "tp"),
            P(None, "tp"),
            P("tp", None),
            P("tp"),
            P("tp"),
            P(),
            P("req"),
            P(),
            P(None, "req", "tp"),
            P("req", None, "tp"),
        ),
        out_specs=(P("req", "tp", None), P("req", None, "tp")),
        check_vma=False,
    )
```

```python
import jax
import jax.numpy as jnp
from jax import lax
from jax.experimental import pallas as pl
from jax.experimental.pallas import tpu as pltpu
from jax.sharding import PartitionSpec as P

HEADS = 8
HD = 128
NEW = 512


def rotate(values_in, positions):
    half_dim = values_in.shape[-1] // 2
    exponent = jnp.arange(half_dim, dtype=jnp.float32) * (-2.0 / values_in.shape[-1])
    inverse = jnp.power(jnp.float32(500000.0), exponent)
    angles = positions[:, None] * inverse[None, :]
    cosine = jnp.cos(angles)[:, None, :]
    sine_part = jnp.sin(angles)[:, None, :]
    first_half = values_in[..., :half_dim]
    second_half = values_in[..., half_dim:]
    return jnp.concatenate(
        [
            first_half * cosine - second_half * sine_part,
            second_half * cosine + first_half * sine_part,
        ],
        -1,
    )


def rms_scale(values_in, gain_vector):
    mean_sq = jnp.mean(values_in * values_in, axis=-1, keepdims=True)
    return values_in * lax.rsqrt(mean_sq + 1e-06) * gain_vector


QUERY_BLOCK = 256
KEY_BLOCK = 512


def attend_kernel(len_ref, q_ref, pre_ref, cache_ref, nk_ref, nv_ref, wo_ref, out_ref, score_ref):
    block = pl.program_id(0)
    length = len_ref[0]
    queries = q_ref[...]
    scale = HD ** (-0.5)
    prefix_chunks = pre_ref.shape[0] // KEY_BLOCK
    cache_chunks = cache_ref.shape[0] // KEY_BLOCK
    row_ids = block * QUERY_BLOCK + lax.broadcasted_iota(jnp.int32, (QUERY_BLOCK, KEY_BLOCK), 0)
    col_ids = lax.broadcasted_iota(jnp.int32, (QUERY_BLOCK, KEY_BLOCK), 1)

    def keys_of(chunk):
        if chunk < prefix_chunks:
            return pre_ref[pl.ds(chunk * KEY_BLOCK, KEY_BLOCK), pl.ds(0, HD)]
        if chunk < prefix_chunks + cache_chunks:
            start = (chunk - prefix_chunks) * KEY_BLOCK
            return cache_ref[pl.ds(start, KEY_BLOCK), pl.ds(0, HD)]
        return nk_ref[...]

    def values_of(chunk):
        if chunk < prefix_chunks:
            return pre_ref[pl.ds(chunk * KEY_BLOCK, KEY_BLOCK), pl.ds(HD, HD)]
        if chunk < prefix_chunks + cache_chunks:
            start = (chunk - prefix_chunks) * KEY_BLOCK
            return cache_ref[pl.ds(start, KEY_BLOCK), pl.ds(HD, HD)]
        return nv_ref[...]

    def visible_of(chunk):
        if chunk < prefix_chunks:
            return None
        if chunk == prefix_chunks:
            return None
        if chunk < prefix_chunks + cache_chunks:
            return col_ids + (chunk - prefix_chunks) * KEY_BLOCK < length
        return col_ids <= row_ids

    chunks = prefix_chunks + cache_chunks + 1
    row_peak = None
    for chunk in range(chunks):
        part = lax.dot_general(
            queries, keys_of(chunk), (((1,), (1,)), ((), ())),
            preferred_element_type=jnp.float32,
        ) * scale
        visible = visible_of(chunk)
        if visible is not None:
            part = jnp.where(visible, part, -1e30)
        score_ref[:, pl.ds(chunk * KEY_BLOCK, KEY_BLOCK)] = part
        peak = jnp.max(part, -1, keepdims=True)
        row_peak = peak if row_peak is None else jnp.maximum(row_peak, peak)
    denominator = jnp.zeros((QUERY_BLOCK, 1), jnp.float32)
    weighted = jnp.zeros((QUERY_BLOCK, HD), jnp.float32)
    for chunk in range(chunks):
        weights = jnp.exp(score_ref[:, pl.ds(chunk * KEY_BLOCK, KEY_BLOCK)] - row_peak)
        denominator = denominator + jnp.sum(weights, -1, keepdims=True)
        weighted = weighted + jnp.dot(
            weights.astype(jnp.bfloat16), values_of(chunk), preferred_element_type=jnp.float32
        )
    attended = (weighted / denominator).astype(jnp.bfloat16)
    out_ref[...] = jnp.dot(
        attended, wo_ref[...], preferred_element_type=jnp.float32
    ).astype(out_ref.dtype)


def attend(cache_lens, queries, prefix_pairs, cache_pairs, keys_new, values_new, w_out):
    new_rows = queries.shape[0]
    whole = lambda block, lens: (0, 0)
    rows = lambda block, lens: (block, 0)
    chunks = (prefix_pairs.shape[0] + cache_pairs.shape[0]) // KEY_BLOCK + 1
    return pl.pallas_call(
        attend_kernel,
        grid_spec=pltpu.PrefetchScalarGridSpec(
            num_scalar_prefetch=1,
            grid=(new_rows // QUERY_BLOCK,),
            in_specs=[
                pl.BlockSpec((QUERY_BLOCK, HD), rows),
                pl.BlockSpec(prefix_pairs.shape, whole),
                pl.BlockSpec(cache_pairs.shape, whole),
                pl.BlockSpec(keys_new.shape, whole),
                pl.BlockSpec(values_new.shape, whole),
                pl.BlockSpec(w_out.shape, whole),
            ],
            out_specs=pl.BlockSpec((QUERY_BLOCK, w_out.shape[1]), rows),
            scratch_shapes=[pltpu.VMEM((QUERY_BLOCK, chunks * KEY_BLOCK), jnp.float32)],
        ),
        out_shape=jax.ShapeDtypeStruct((new_rows, w_out.shape[1]), jnp.bfloat16),
        compiler_params=pltpu.CompilerParams(dimension_semantics=("arbitrary",)),
    )(cache_lens, queries, prefix_pairs, cache_pairs, keys_new, values_new, w_out)


def layer(
    tokens,
    w_q,
    w_k,
    w_v,
    w_o,
    q_gain,
    k_gain,
    out_gain,
    cache_lens,
    group_ids,
    prefix_cache,
    cache_rows,
):
    heads_local = w_q.shape[1] // HD
    tp_size = lax.axis_size("tp")
    flat_rows = lax.all_to_all(
        jnp.broadcast_to(tokens, (tp_size,) + tokens.shape[1:]), "tp", 0, 0, tiled=True
    ).reshape(-1, tokens.shape[2])
    outgoing = jnp.take(prefix_cache, group_ids, axis=0)
    chosen = lax.all_to_all(outgoing, "req", 0, 0, tiled=True)
    queries = jnp.dot(flat_rows, w_q, preferred_element_type=jnp.float32)
    keys_new = jnp.dot(flat_rows, w_k, preferred_element_type=jnp.float32)
    values_new = jnp.dot(flat_rows, w_v, preferred_element_type=jnp.float32)
    square_sums = lax.psum((jnp.sum(queries * queries, -1), jnp.sum(keys_new * keys_new, -1)), "tp")
    full_width = HEADS * HD
    queries = queries * lax.rsqrt(square_sums[0] / full_width + 1e-06)[:, None] * q_gain
    keys_new = keys_new * lax.rsqrt(square_sums[1] / full_width + 1e-06)[:, None] * k_gain
    prefix_len = prefix_cache.shape[1] * lax.axis_size("req")
    length = cache_lens[0]
    positions = (prefix_len + length + jnp.arange(NEW, dtype=jnp.int32)).astype(jnp.float32)
    q_rot = rotate(queries.reshape(NEW, heads_local, HD), positions).astype(jnp.bfloat16)
    k_rot = rotate(keys_new.reshape(NEW, heads_local, HD), positions).astype(jnp.bfloat16)
    v_new = values_new.reshape(NEW, heads_local, HD).astype(jnp.bfloat16)
    appended = jnp.stack([k_rot, v_new], axis=2).reshape(1, NEW, heads_local * 2 * HD)

    shared = chosen.reshape(-1, heads_local * 2 * HD)
    cached = cache_rows[0]
    partial_sum = None
    for head in range(heads_local):
        pair = slice(head * 2 * HD, (head + 1) * 2 * HD)
        partial = attend(
            cache_lens,
            q_rot[:, head],
            shared[:, pair],
            cached[:, pair],
            k_rot[:, head],
            v_new[:, head],
            w_o[head * HD : (head + 1) * HD],
        )
        partial = partial if heads_local == 1 else partial.astype(jnp.float32)
        partial_sum = partial if partial_sum is None else partial_sum + partial
    partial_out = partial_sum.astype(jnp.bfloat16)
    blocks_out = partial_out.astype(jnp.bfloat16).reshape(tp_size, -1, partial_out.shape[1])
    mine = jnp.sum(lax.all_to_all(blocks_out, "tp", 0, 0, tiled=True).astype(jnp.float32), 0)
    hidden = (tokens[0].astype(jnp.float32) + rms_scale(mine, out_gain)).astype(jnp.bfloat16)[None]
    return (hidden, appended)


def solution(mesh):
    return jax.shard_map(
        layer,
        mesh=mesh,
        in_specs=(
            P("req", "tp", None),
            P(None, "tp"),
            P(None, "tp"),
            P(None, "tp"),
            P("tp", None),
            P("tp"),
            P("tp"),
            P(),
            P("req"),
            P(),
            P(None, "req", "tp"),
            P("req", None, "tp"),
        ),
        out_specs=(P("req", "tp", None), P("req", None, "tp")),
        check_vma=False,
    )
```

```python
import jax
import jax.numpy as jnp
from jax import lax
from jax.experimental import pallas as pl
from jax.experimental.pallas import tpu as pltpu
from jax.sharding import PartitionSpec as P

HEADS = 8
HD = 128
NEW = 512


def rotate(values_in, positions):
    half_dim = values_in.shape[-1] // 2
    exponent = jnp.arange(half_dim, dtype=jnp.float32) * (-2.0 / values_in.shape[-1])
    inverse = jnp.power(jnp.float32(500000.0), exponent)
    angles = positions[:, None] * inverse[None, :]
    cosine = jnp.cos(angles)[:, None, :]
    sine_part = jnp.sin(angles)[:, None, :]
    first_half = values_in[..., :half_dim]
    second_half = values_in[..., half_dim:]
    return jnp.concatenate(
        [
            first_half * cosine - second_half * sine_part,
            second_half * cosine + first_half * sine_part,
        ],
        -1,
    )


def rms_scale(values_in, gain_vector):
    mean_sq = jnp.mean(values_in * values_in, axis=-1, keepdims=True)
    return values_in * lax.rsqrt(mean_sq + 1e-06) * gain_vector


QUERY_BLOCK = 256
KEY_BLOCK = 512


def attend_kernel(len_ref, q_ref, pre_ref, cache_ref, nk_ref, nv_ref, wo_ref, out_ref, score_ref):
    block = pl.program_id(0)
    length = len_ref[0]
    queries = q_ref[...]
    scale = HD ** (-0.5)
    prefix_chunks = pre_ref.shape[0] // KEY_BLOCK
    cache_chunks = cache_ref.shape[0] // KEY_BLOCK
    row_ids = block * QUERY_BLOCK + lax.broadcasted_iota(jnp.int32, (QUERY_BLOCK, KEY_BLOCK), 0)
    col_ids = lax.broadcasted_iota(jnp.int32, (QUERY_BLOCK, KEY_BLOCK), 1)

    def keys_of(chunk):
        if chunk < prefix_chunks:
            return pre_ref[pl.ds(chunk * KEY_BLOCK, KEY_BLOCK), pl.ds(0, HD)]
        if chunk < prefix_chunks + cache_chunks:
            start = (chunk - prefix_chunks) * KEY_BLOCK
            return cache_ref[pl.ds(start, KEY_BLOCK), pl.ds(0, HD)]
        return nk_ref[...]

    def values_of(chunk):
        if chunk < prefix_chunks:
            return pre_ref[pl.ds(chunk * KEY_BLOCK, KEY_BLOCK), pl.ds(HD, HD)]
        if chunk < prefix_chunks + cache_chunks:
            start = (chunk - prefix_chunks) * KEY_BLOCK
            return cache_ref[pl.ds(start, KEY_BLOCK), pl.ds(HD, HD)]
        return nv_ref[...]

    def visible_of(chunk):
        if chunk < prefix_chunks:
            return None
        if chunk == prefix_chunks:
            return None
        if chunk < prefix_chunks + cache_chunks:
            return col_ids + (chunk - prefix_chunks) * KEY_BLOCK < length
        return col_ids <= row_ids

    chunks = prefix_chunks + cache_chunks + 1
    row_peak = None
    for chunk in range(chunks):
        part = lax.dot_general(
            queries, keys_of(chunk), (((1,), (1,)), ((), ())),
            preferred_element_type=jnp.float32,
        ) * scale
        visible = visible_of(chunk)
        if visible is not None:
            part = jnp.where(visible, part, -1e30)
        score_ref[:, pl.ds(chunk * KEY_BLOCK, KEY_BLOCK)] = part
        peak = jnp.max(part, -1, keepdims=True)
        row_peak = peak if row_peak is None else jnp.maximum(row_peak, peak)
    denominator = jnp.zeros((QUERY_BLOCK, 1), jnp.float32)
    weighted = jnp.zeros((QUERY_BLOCK, HD), jnp.float32)
    for chunk in range(chunks):
        weights = jnp.exp(score_ref[:, pl.ds(chunk * KEY_BLOCK, KEY_BLOCK)] - row_peak)
        denominator = denominator + jnp.sum(weights, -1, keepdims=True)
        weighted = weighted + jnp.dot(
            weights.astype(jnp.bfloat16), values_of(chunk), preferred_element_type=jnp.float32
        )
    attended = (weighted / denominator).astype(jnp.bfloat16)
    out_ref[...] = jnp.dot(
        attended, wo_ref[...], preferred_element_type=jnp.float32
    ).astype(out_ref.dtype)


def attend(cache_lens, queries, prefix_pairs, cache_pairs, keys_new, values_new, w_out):
    new_rows = queries.shape[0]
    whole = lambda block, lens: (0, 0)
    rows = lambda block, lens: (block, 0)
    chunks = (prefix_pairs.shape[0] + cache_pairs.shape[0]) // KEY_BLOCK + 1
    return pl.pallas_call(
        attend_kernel,
        grid_spec=pltpu.PrefetchScalarGridSpec(
            num_scalar_prefetch=1,
            grid=(new_rows // QUERY_BLOCK,),
            in_specs=[
                pl.BlockSpec((QUERY_BLOCK, HD), rows),
                pl.BlockSpec(prefix_pairs.shape, whole),
                pl.BlockSpec(cache_pairs.shape, whole),
                pl.BlockSpec(keys_new.shape, whole),
                pl.BlockSpec(values_new.shape, whole),
                pl.BlockSpec(w_out.shape, whole),
            ],
            out_specs=pl.BlockSpec((QUERY_BLOCK, w_out.shape[1]), rows),
            scratch_shapes=[pltpu.VMEM((QUERY_BLOCK, chunks * KEY_BLOCK), jnp.float32)],
        ),
        out_shape=jax.ShapeDtypeStruct((new_rows, w_out.shape[1]), jnp.bfloat16),
        compiler_params=pltpu.CompilerParams(dimension_semantics=("arbitrary",)),
    )(cache_lens, queries, prefix_pairs, cache_pairs, keys_new, values_new, w_out)


def repeat_kernel(in_ref, out_ref, sems):
    copies = [
        pltpu.make_async_copy(in_ref, out_ref.at[pl.ds(i, 1)], sems.at[i])
        for i in range(out_ref.shape[0])
    ]
    for copy in copies:
        copy.start()
    for copy in copies:
        copy.wait()


def repeat_rows(block, copies):
    return pl.pallas_call(
        repeat_kernel,
        in_specs=[pl.BlockSpec(memory_space=pltpu.VMEM)],
        out_specs=pl.BlockSpec(memory_space=pl.ANY),
        out_shape=jax.ShapeDtypeStruct((copies,) + block.shape[1:], block.dtype),
        scratch_shapes=[pltpu.SemaphoreType.DMA((copies,))],
    )(block)


def layer(
    tokens,
    w_q,
    w_k,
    w_v,
    w_o,
    q_gain,
    k_gain,
    out_gain,
    cache_lens,
    group_ids,
    prefix_cache,
    cache_rows,
):
    heads_local = w_q.shape[1] // HD
    tp_size = lax.axis_size("tp")
    flat_rows = lax.all_to_all(
        repeat_rows(tokens, tp_size), "tp", 0, 0, tiled=True
    ).reshape(-1, tokens.shape[2])
    outgoing = jnp.take(prefix_cache, group_ids, axis=0)
    chosen = lax.all_to_all(outgoing, "req", 0, 0, tiled=True)
    queries = jnp.dot(flat_rows, w_q, preferred_element_type=jnp.float32)
    keys_new = jnp.dot(flat_rows, w_k, preferred_element_type=jnp.float32)
    values_new = jnp.dot(flat_rows, w_v, preferred_element_type=jnp.float32)
    square_sums = lax.psum((jnp.sum(queries * queries, -1), jnp.sum(keys_new * keys_new, -1)), "tp")
    full_width = HEADS * HD
    queries = queries * lax.rsqrt(square_sums[0] / full_width + 1e-06)[:, None] * q_gain
    keys_new = keys_new * lax.rsqrt(square_sums[1] / full_width + 1e-06)[:, None] * k_gain
    prefix_len = prefix_cache.shape[1] * lax.axis_size("req")
    length = cache_lens[0]
    positions = (prefix_len + length + jnp.arange(NEW, dtype=jnp.int32)).astype(jnp.float32)
    q_rot = rotate(queries.reshape(NEW, heads_local, HD), positions).astype(jnp.bfloat16)
    k_rot = rotate(keys_new.reshape(NEW, heads_local, HD), positions).astype(jnp.bfloat16)
    v_new = values_new.reshape(NEW, heads_local, HD).astype(jnp.bfloat16)
    appended = jnp.stack([k_rot, v_new], axis=2).reshape(1, NEW, heads_local * 2 * HD)

    shared = chosen.reshape(-1, heads_local * 2 * HD)
    cached = cache_rows[0]
    partial_sum = None
    for head in range(heads_local):
        pair = slice(head * 2 * HD, (head + 1) * 2 * HD)
        partial = attend(
            cache_lens,
            q_rot[:, head],
            shared[:, pair],
            cached[:, pair],
            k_rot[:, head],
            v_new[:, head],
            w_o[head * HD : (head + 1) * HD],
        )
        partial = partial if heads_local == 1 else partial.astype(jnp.float32)
        partial_sum = partial if partial_sum is None else partial_sum + partial
    partial_out = partial_sum.astype(jnp.bfloat16)
    blocks_out = partial_out.astype(jnp.bfloat16).reshape(tp_size, -1, partial_out.shape[1])
    mine = jnp.sum(lax.all_to_all(blocks_out, "tp", 0, 0, tiled=True).astype(jnp.float32), 0)
    hidden = (tokens[0].astype(jnp.float32) + rms_scale(mine, out_gain)).astype(jnp.bfloat16)[None]
    return (hidden, appended)


def solution(mesh):
    return jax.shard_map(
        layer,
        mesh=mesh,
        in_specs=(
            P("req", "tp", None),
            P(None, "tp"),
            P(None, "tp"),
            P(None, "tp"),
            P("tp", None),
            P("tp"),
            P("tp"),
            P(),
            P("req"),
            P(),
            P(None, "req", "tp"),
            P("req", None, "tp"),
        ),
        out_specs=(P("req", "tp", None), P("req", None, "tp")),
        check_vma=False,
    )
```

```python
import jax
import jax.numpy as jnp
from jax import lax
from jax.experimental import pallas as pl
from jax.experimental.pallas import tpu as pltpu
from jax.sharding import PartitionSpec as P


HEADS = 8
HD = 128
NEW = 512


def rotate(values_in, positions):
    half_dim = values_in.shape[-1] // 2
    exponent = jnp.arange(half_dim, dtype=jnp.float32) * (-2.0 / values_in.shape[-1])
    inverse = jnp.power(jnp.float32(500000.0), exponent)
    angles = positions[:, None] * inverse[None, :]
    cosine = jnp.cos(angles)[:, None, :]
    sine_part = jnp.sin(angles)[:, None, :]
    first_half = values_in[..., :half_dim]
    second_half = values_in[..., half_dim:]
    return jnp.concatenate(
        [
            first_half * cosine - second_half * sine_part,
            second_half * cosine + first_half * sine_part,
        ],
        -1,
    )


def rms_scale(values_in, gain_vector):
    mean_sq = jnp.mean(values_in * values_in, axis=-1, keepdims=True)
    return values_in * lax.rsqrt(mean_sq + 1e-06) * gain_vector


QUERY_BLOCK = 256
KEY_BLOCK = 512


def scores_of(queries, keys):
    return lax.dot_general(
        queries, keys, (((1,), (1,)), ((), ())), preferred_element_type=jnp.float32
    ) * HD ** (-0.5)


def private_kernel(len_ref, q_ref, cache_ref, nk_ref, nv_ref, peak_ref, sum_ref, acc_ref, score_ref):
    block = pl.program_id(0)
    length = len_ref[0]
    queries = q_ref[...]
    cache_chunks = cache_ref.shape[0] // KEY_BLOCK
    row_ids = block * QUERY_BLOCK + lax.broadcasted_iota(jnp.int32, (QUERY_BLOCK, KEY_BLOCK), 0)
    col_ids = lax.broadcasted_iota(jnp.int32, (QUERY_BLOCK, KEY_BLOCK), 1)
    row_peak = None
    for chunk in range(cache_chunks + 1):
        if chunk < cache_chunks:
            part = scores_of(queries, cache_ref[pl.ds(chunk * KEY_BLOCK, KEY_BLOCK), pl.ds(0, HD)])
            if chunk > 0:
                part = jnp.where(col_ids + chunk * KEY_BLOCK < length, part, -1e30)
        else:
            part = jnp.where(col_ids <= row_ids, scores_of(queries, nk_ref[...]), -1e30)
        score_ref[:, pl.ds(chunk * KEY_BLOCK, KEY_BLOCK)] = part
        peak = jnp.max(part, -1, keepdims=True)
        row_peak = peak if row_peak is None else jnp.maximum(row_peak, peak)
    denominator = jnp.zeros((QUERY_BLOCK, 1), jnp.float32)
    weighted = jnp.zeros((QUERY_BLOCK, HD), jnp.float32)
    for chunk in range(cache_chunks + 1):
        weights = jnp.exp(score_ref[:, pl.ds(chunk * KEY_BLOCK, KEY_BLOCK)] - row_peak)
        if chunk < cache_chunks:
            values = cache_ref[pl.ds(chunk * KEY_BLOCK, KEY_BLOCK), pl.ds(HD, HD)]
        else:
            values = nv_ref[...]
        denominator = denominator + jnp.sum(weights, -1, keepdims=True)
        weighted = weighted + jnp.dot(
            weights.astype(jnp.bfloat16), values, preferred_element_type=jnp.float32
        )
    peak_ref[...] = jnp.broadcast_to(row_peak, peak_ref.shape)
    sum_ref[...] = jnp.broadcast_to(denominator, sum_ref.shape)
    acc_ref[...] = weighted


def shared_kernel(q_ref, pre_ref, peak_ref, sum_ref, acc_ref, wo_ref, out_ref, score_ref):
    queries = q_ref[...]
    prefix_chunks = pre_ref.shape[0] // KEY_BLOCK
    old_peak = peak_ref[:, :1]
    row_peak = old_peak
    for chunk in range(prefix_chunks):
        part = scores_of(queries, pre_ref[pl.ds(chunk * KEY_BLOCK, KEY_BLOCK), pl.ds(0, HD)])
        score_ref[:, pl.ds(chunk * KEY_BLOCK, KEY_BLOCK)] = part
        row_peak = jnp.maximum(row_peak, jnp.max(part, -1, keepdims=True))
    rescale = jnp.exp(old_peak - row_peak)
    denominator = sum_ref[:, :1] * rescale
    weighted = acc_ref[...] * rescale
    for chunk in range(prefix_chunks):
        weights = jnp.exp(score_ref[:, pl.ds(chunk * KEY_BLOCK, KEY_BLOCK)] - row_peak)
        denominator = denominator + jnp.sum(weights, -1, keepdims=True)
        weighted = weighted + jnp.dot(
            weights.astype(jnp.bfloat16),
            pre_ref[pl.ds(chunk * KEY_BLOCK, KEY_BLOCK), pl.ds(HD, HD)],
            preferred_element_type=jnp.float32,
        )
    attended = (weighted / denominator).astype(jnp.bfloat16)
    out_ref[...] = jnp.dot(
        attended, wo_ref[...], preferred_element_type=jnp.float32
    ).astype(out_ref.dtype)


def attend(cache_lens, queries, prefix_pairs, cache_pairs, keys_new, values_new, w_out):
    new_rows = queries.shape[0]
    whole = lambda block, *rest: (0, 0)
    rows = lambda block, *rest: (block, 0)
    grid = (new_rows // QUERY_BLOCK,)
    row_block = pl.BlockSpec((QUERY_BLOCK, HD), rows)
    state = jax.ShapeDtypeStruct((new_rows, HD), jnp.float32)
    peak, total, acc = pl.pallas_call(
        private_kernel,
        grid_spec=pltpu.PrefetchScalarGridSpec(
            num_scalar_prefetch=1,
            grid=grid,
            in_specs=[
                row_block,
                pl.BlockSpec(cache_pairs.shape, whole),
                pl.BlockSpec(keys_new.shape, whole),
                pl.BlockSpec(values_new.shape, whole),
            ],
            out_specs=[row_block, row_block, row_block],
            scratch_shapes=[
                pltpu.VMEM((QUERY_BLOCK, cache_pairs.shape[0] + KEY_BLOCK), jnp.float32)
            ],
        ),
        out_shape=[state, state, state],
        compiler_params=pltpu.CompilerParams(dimension_semantics=("arbitrary",)),
    )(cache_lens, queries, cache_pairs, keys_new, values_new)
    return pl.pallas_call(
        shared_kernel,
        grid=grid,
        in_specs=[
            row_block,
            pl.BlockSpec(prefix_pairs.shape, whole),
            row_block,
            row_block,
            row_block,
            pl.BlockSpec(w_out.shape, whole),
        ],
        out_specs=pl.BlockSpec((QUERY_BLOCK, w_out.shape[1]), rows),
        out_shape=jax.ShapeDtypeStruct((new_rows, w_out.shape[1]), jnp.bfloat16),
        scratch_shapes=[pltpu.VMEM((QUERY_BLOCK, prefix_pairs.shape[0]), jnp.float32)],
        compiler_params=pltpu.CompilerParams(dimension_semantics=("arbitrary",)),
    )(queries, prefix_pairs, peak, total, acc, w_out)


def layer(
    tokens,
    w_q,
    w_k,
    w_v,
    w_o,
    q_gain,
    k_gain,
    out_gain,
    cache_lens,
    group_ids,
    prefix_cache,
    cache_rows,
):
    heads_local = w_q.shape[1] // HD
    tp_size = lax.axis_size("tp")
    flat_rows = lax.all_to_all(
        jnp.broadcast_to(tokens, (tp_size,) + tokens.shape[1:]), "tp", 0, 0, tiled=True
    ).reshape(-1, tokens.shape[2])
    outgoing = jnp.take(prefix_cache, group_ids, axis=0)
    chosen = lax.all_to_all(outgoing, "req", 0, 0, tiled=True)
    queries = jnp.dot(flat_rows, w_q, preferred_element_type=jnp.float32)
    keys_new = jnp.dot(flat_rows, w_k, preferred_element_type=jnp.float32)
    values_new = jnp.dot(flat_rows, w_v, preferred_element_type=jnp.float32)
    square_sums = lax.psum((jnp.sum(queries * queries, -1), jnp.sum(keys_new * keys_new, -1)), "tp")
    full_width = HEADS * HD
    queries = queries * lax.rsqrt(square_sums[0] / full_width + 1e-06)[:, None] * q_gain
    keys_new = keys_new * lax.rsqrt(square_sums[1] / full_width + 1e-06)[:, None] * k_gain
    prefix_len = prefix_cache.shape[1] * lax.axis_size("req")
    length = cache_lens[0]
    positions = (prefix_len + length + jnp.arange(NEW, dtype=jnp.int32)).astype(jnp.float32)
    q_rot = rotate(queries.reshape(NEW, heads_local, HD), positions).astype(jnp.bfloat16)
    k_rot = rotate(keys_new.reshape(NEW, heads_local, HD), positions).astype(jnp.bfloat16)
    v_new = values_new.reshape(NEW, heads_local, HD).astype(jnp.bfloat16)
    appended = jnp.stack([k_rot, v_new], axis=2).reshape(1, NEW, heads_local * 2 * HD)

    shared = chosen.reshape(-1, heads_local * 2 * HD)
    cached = cache_rows[0]
    partial_sum = None
    for head in range(heads_local):
        pair = slice(head * 2 * HD, (head + 1) * 2 * HD)
        partial = attend(
            cache_lens,
            q_rot[:, head],
            shared[:, pair],
            cached[:, pair],
            k_rot[:, head],
            v_new[:, head],
            w_o[head * HD : (head + 1) * HD],
        )
        partial = partial if heads_local == 1 else partial.astype(jnp.float32)
        partial_sum = partial if partial_sum is None else partial_sum + partial
    partial_out = partial_sum.astype(jnp.bfloat16)
    blocks_out = partial_out.astype(jnp.bfloat16).reshape(tp_size, -1, partial_out.shape[1])
    received = lax.all_to_all(blocks_out, "tp", 0, 0, tiled=True)
    mine = jnp.sum(received.astype(jnp.float32), 0)
    hidden = (tokens[0].astype(jnp.float32) + rms_scale(mine, out_gain)).astype(jnp.bfloat16)[None]
    return (hidden, appended)


def solution(mesh):
    return jax.shard_map(
        layer,
        mesh=mesh,
        in_specs=(
            P("req", "tp", None),
            P(None, "tp"),
            P(None, "tp"),
            P(None, "tp"),
            P("tp", None),
            P("tp"),
            P("tp"),
            P(),
            P("req"),
            P(),
            P(None, "req", "tp"),
            P("req", None, "tp"),
        ),
        out_specs=(P("req", "tp", None), P("req", None, "tp")),
        check_vma=False,
    )
```

```python
import jax
import jax.numpy as jnp
from jax import lax
from jax.experimental import pallas as pl
from jax.experimental.pallas import tpu as pltpu
from jax.sharding import PartitionSpec as P

HEADS = 8
HD = 128
NEW = 512


def rotate(values_in, positions):
    half_dim = values_in.shape[-1] // 2
    exponent = jnp.arange(half_dim, dtype=jnp.float32) * (-2.0 / values_in.shape[-1])
    inverse = jnp.power(jnp.float32(500000.0), exponent)
    angles = positions[:, None] * inverse[None, :]
    cosine = jnp.cos(angles)[:, None, :]
    sine_part = jnp.sin(angles)[:, None, :]
    first_half = values_in[..., :half_dim]
    second_half = values_in[..., half_dim:]
    return jnp.concatenate(
        [
            first_half * cosine - second_half * sine_part,
            second_half * cosine + first_half * sine_part,
        ],
        -1,
    )


def rms_scale(values_in, gain_vector):
    mean_sq = jnp.mean(values_in * values_in, axis=-1, keepdims=True)
    return values_in * lax.rsqrt(mean_sq + 1e-06) * gain_vector


QUERY_BLOCK = 256
KEY_BLOCK = 512


def scores_of(queries, keys):
    return lax.dot_general(
        queries, keys, (((1,), (1,)), ((), ())), preferred_element_type=jnp.float32
    ) * HD ** (-0.5)


def private_kernel(len_ref, q_ref, cache_ref, nk_ref, nv_ref, stat_ref, acc_ref, score_ref):
    block = pl.program_id(0)
    length = len_ref[0]
    queries = q_ref[...]
    cache_chunks = cache_ref.shape[0] // KEY_BLOCK
    row_ids = block * QUERY_BLOCK + lax.broadcasted_iota(jnp.int32, (QUERY_BLOCK, KEY_BLOCK), 0)
    col_ids = lax.broadcasted_iota(jnp.int32, (QUERY_BLOCK, KEY_BLOCK), 1)
    row_peak = None
    for chunk in range(cache_chunks + 1):
        if chunk < cache_chunks:
            part = scores_of(queries, cache_ref[pl.ds(chunk * KEY_BLOCK, KEY_BLOCK), pl.ds(0, HD)])
            if chunk > 0:
                part = jnp.where(col_ids + chunk * KEY_BLOCK < length, part, -1e30)
        else:
            part = jnp.where(col_ids <= row_ids, scores_of(queries, nk_ref[...]), -1e30)
        score_ref[:, pl.ds(chunk * KEY_BLOCK, KEY_BLOCK)] = part
        peak = jnp.max(part, -1, keepdims=True)
        row_peak = peak if row_peak is None else jnp.maximum(row_peak, peak)
    denominator = jnp.zeros((QUERY_BLOCK, 1), jnp.float32)
    weighted = jnp.zeros((QUERY_BLOCK, HD), jnp.float32)
    for chunk in range(cache_chunks + 1):
        weights = jnp.exp(score_ref[:, pl.ds(chunk * KEY_BLOCK, KEY_BLOCK)] - row_peak)
        if chunk < cache_chunks:
            values = cache_ref[pl.ds(chunk * KEY_BLOCK, KEY_BLOCK), pl.ds(HD, HD)]
        else:
            values = nv_ref[...]
        denominator = denominator + jnp.sum(weights, -1, keepdims=True)
        weighted = weighted + jnp.dot(
            weights.astype(jnp.bfloat16), values, preferred_element_type=jnp.float32
        )
    lane = lax.broadcasted_iota(jnp.int32, stat_ref.shape, 1)
    stat_ref[...] = jnp.where(lane == 0, row_peak, denominator)
    acc_ref[...] = weighted


def shared_kernel(q_ref, pre_ref, stat_ref, acc_ref, wo_ref, out_ref, score_ref):
    queries = q_ref[...]
    prefix_chunks = pre_ref.shape[0] // KEY_BLOCK
    old_peak = stat_ref[:, :1]
    row_peak = old_peak
    for chunk in range(prefix_chunks):
        part = scores_of(queries, pre_ref[pl.ds(chunk * KEY_BLOCK, KEY_BLOCK), pl.ds(0, HD)])
        score_ref[:, pl.ds(chunk * KEY_BLOCK, KEY_BLOCK)] = part
        row_peak = jnp.maximum(row_peak, jnp.max(part, -1, keepdims=True))
    rescale = jnp.exp(old_peak - row_peak)
    denominator = stat_ref[:, 1:2] * rescale
    weighted = acc_ref[...] * rescale
    for chunk in range(prefix_chunks):
        weights = jnp.exp(score_ref[:, pl.ds(chunk * KEY_BLOCK, KEY_BLOCK)] - row_peak)
        denominator = denominator + jnp.sum(weights, -1, keepdims=True)
        weighted = weighted + jnp.dot(
            weights.astype(jnp.bfloat16),
            pre_ref[pl.ds(chunk * KEY_BLOCK, KEY_BLOCK), pl.ds(HD, HD)],
            preferred_element_type=jnp.float32,
        )
    attended = (weighted / denominator).astype(jnp.bfloat16)
    out_ref[...] = jnp.dot(
        attended, wo_ref[...], preferred_element_type=jnp.float32
    ).astype(out_ref.dtype)


def attend(cache_lens, queries, prefix_pairs, cache_pairs, keys_new, values_new, w_out):
    new_rows = queries.shape[0]
    whole = lambda block, *rest: (0, 0)
    rows = lambda block, *rest: (block, 0)
    grid = (new_rows // QUERY_BLOCK,)
    row_block = pl.BlockSpec((QUERY_BLOCK, HD), rows)
    state = jax.ShapeDtypeStruct((new_rows, HD), jnp.float32)
    stats, acc = pl.pallas_call(
        private_kernel,
        grid_spec=pltpu.PrefetchScalarGridSpec(
            num_scalar_prefetch=1,
            grid=grid,
            in_specs=[
                row_block,
                pl.BlockSpec(cache_pairs.shape, whole),
                pl.BlockSpec(keys_new.shape, whole),
                pl.BlockSpec(values_new.shape, whole),
            ],
            out_specs=[row_block, row_block],
            scratch_shapes=[
                pltpu.VMEM((QUERY_BLOCK, cache_pairs.shape[0] + KEY_BLOCK), jnp.float32)
            ],
        ),
        out_shape=[state, state],
        compiler_params=pltpu.CompilerParams(dimension_semantics=("arbitrary",)),
    )(cache_lens, queries, cache_pairs, keys_new, values_new)
    return pl.pallas_call(
        shared_kernel,
        grid=grid,
        in_specs=[
            row_block,
            pl.BlockSpec(prefix_pairs.shape, whole),
            row_block,
            row_block,
            pl.BlockSpec(w_out.shape, whole),
        ],
        out_specs=pl.BlockSpec((QUERY_BLOCK, w_out.shape[1]), rows),
        out_shape=jax.ShapeDtypeStruct((new_rows, w_out.shape[1]), jnp.bfloat16),
        scratch_shapes=[pltpu.VMEM((QUERY_BLOCK, prefix_pairs.shape[0]), jnp.float32)],
        compiler_params=pltpu.CompilerParams(dimension_semantics=("arbitrary",)),
    )(queries, prefix_pairs, stats, acc, w_out)


def layer(
    tokens,
    w_q,
    w_k,
    w_v,
    w_o,
    q_gain,
    k_gain,
    out_gain,
    cache_lens,
    group_ids,
    prefix_cache,
    cache_rows,
):
    heads_local = w_q.shape[1] // HD
    tp_size = lax.axis_size("tp")
    flat_rows = lax.all_to_all(
        jnp.broadcast_to(tokens, (tp_size,) + tokens.shape[1:]), "tp", 0, 0, tiled=True
    ).reshape(-1, tokens.shape[2])
    outgoing = jnp.take(prefix_cache, group_ids, axis=0)
    chosen = lax.all_to_all(outgoing, "req", 0, 0, tiled=True)
    queries = jnp.dot(flat_rows, w_q, preferred_element_type=jnp.float32)
    keys_new = jnp.dot(flat_rows, w_k, preferred_element_type=jnp.float32)
    values_new = jnp.dot(flat_rows, w_v, preferred_element_type=jnp.float32)
    square_sums = lax.psum((jnp.sum(queries * queries, -1), jnp.sum(keys_new * keys_new, -1)), "tp")
    full_width = HEADS * HD
    queries = queries * lax.rsqrt(square_sums[0] / full_width + 1e-06)[:, None] * q_gain
    keys_new = keys_new * lax.rsqrt(square_sums[1] / full_width + 1e-06)[:, None] * k_gain
    prefix_len = prefix_cache.shape[1] * lax.axis_size("req")
    length = cache_lens[0]
    positions = (prefix_len + length + jnp.arange(NEW, dtype=jnp.int32)).astype(jnp.float32)
    q_rot = rotate(queries.reshape(NEW, heads_local, HD), positions).astype(jnp.bfloat16)
    k_rot = rotate(keys_new.reshape(NEW, heads_local, HD), positions).astype(jnp.bfloat16)
    v_new = values_new.reshape(NEW, heads_local, HD).astype(jnp.bfloat16)
    appended = jnp.stack([k_rot, v_new], axis=2).reshape(1, NEW, heads_local * 2 * HD)

    shared = chosen.reshape(-1, heads_local * 2 * HD)
    cached = cache_rows[0]
    partial_sum = None
    for head in range(heads_local):
        pair = slice(head * 2 * HD, (head + 1) * 2 * HD)
        partial = attend(
            cache_lens,
            q_rot[:, head],
            shared[:, pair],
            cached[:, pair],
            k_rot[:, head],
            v_new[:, head],
            w_o[head * HD : (head + 1) * HD],
        )
        partial = partial if heads_local == 1 else partial.astype(jnp.float32)
        partial_sum = partial if partial_sum is None else partial_sum + partial
    partial_out = partial_sum.astype(jnp.bfloat16)
    blocks_out = partial_out.astype(jnp.bfloat16).reshape(tp_size, -1, partial_out.shape[1])
    mine = jnp.sum(lax.all_to_all(blocks_out, "tp", 0, 0, tiled=True).astype(jnp.float32), 0)
    hidden = (tokens[0].astype(jnp.float32) + rms_scale(mine, out_gain)).astype(jnp.bfloat16)[None]
    return (hidden, appended)


def solution(mesh):
    return jax.shard_map(
        layer,
        mesh=mesh,
        in_specs=(
            P("req", "tp", None),
            P(None, "tp"),
            P(None, "tp"),
            P(None, "tp"),
            P("tp", None),
            P("tp"),
            P("tp"),
            P(),
            P("req"),
            P(),
            P(None, "req", "tp"),
            P("req", None, "tp"),
        ),
        out_specs=(P("req", "tp", None), P("req", None, "tp")),
        check_vma=False,
    )
```
